128 devices in a mesh: ctx: 32 (over y, z, x_lo), tp: 4 (over x_hi, core).
Axes of the slice: x: 4 (x_hi: 2, x_lo: 2; x = x_hi * 2 + x_lo), y: 4, z: 4, core: 2. Of those that a mesh axis runs over, the one named last changes fastest.
Arguments:
- queries: bfloat16 [16384, 2048], P('ctx', 'tp'), may hold values from -7 to 7
- keys: bfloat16 [16384, 2048], P('ctx', 'tp'), may hold values from -6 to 6
- values: bfloat16 [16384, 2048], P('ctx', 'tp'), may hold values from -6 to 6
- doc_ids: int32 [128], replicated, may hold values from 0 to 15, never falling along the last dimension, each value on 1 to 80 neighbouring positions
- span_start: int32 [16], replicated, may hold values from 0 to 127, as said below
- span_end: int32 [16], replicated, may hold values from 1 to 128, as said below
- out_weight: bfloat16 [2048, 4096], P('tp'), may hold values from -0.125 to 0.125
Outputs:
- mixed: bfloat16 [16384, 4096], P(('ctx', 'tp'))
The draws below stay inside these ranges and needn't reach their ends.
Inputs may be any that keep to these rules, and one draw needn't show every extreme that they name: `doc_ids`: each document occupies consecutive blocks. Spans are disjoint and in increasing order; span s covers blocks span_start[s] to span_end[s] - 1. span_end[s] - span_start[s] is 1 to 4.
All inputs are finite; a program needn't handle non-finite values.
Results may differ from the reference program's by a relative error of at most 0.012.
Values may be sent and summed in bfloat16 or wider, within the bound.
No kernel may reach another device: no remote copies, remote signals or barrier semaphores. Data moves between devices by JAX's collectives and lax.ppermute only.
A program may use at most 128 MiB of HBM per device.

```python
import math
import jax
import jax.numpy as jnp
import numpy as np
from jax import lax

D = 4096
HEADS = 16
HEAD_DIM = 128
BLOCK = 128
SEQ = 16384
NB = 128
NDOC = 16
DOC_MOST = 80


def attention_pair(key):
    base = jax.random.fold_in(key, 5)
    key_one, key_two = jax.random.split(base, 2)
    shape = (SEQ, HEADS * HEAD_DIM)
    query_draw = jnp.clip(jax.random.normal(key_one, shape, jnp.float32), -6.0, 6.0)
    key_draw = jnp.clip(jax.random.normal(key_two, shape, jnp.float32), -6.0, 6.0)
    return (query_draw, key_draw)


def draw_queries(key, part):
    return attention_pair(key)[0].astype(jnp.bfloat16)


def draw_keys(key, part):
    return attention_pair(key)[1].astype(jnp.bfloat16)


def span_pair(key):
    base = jax.random.fold_in(key, 11)
    key_offset, key_length = jax.random.split(base)
    groups = NB // 8
    offset = jax.random.randint(key_offset, (groups,), 0, 4)
    length = jax.random.randint(key_length, (groups,), 1, 5)
    group = jnp.arange(groups, dtype=jnp.int32)
    offset = jnp.where(group == 0, 0, offset)
    length = jnp.where(group == 0, 4, length)
    start = 8 * group + offset
    start = jnp.where(group == groups - 1, 8 * group + 8 - length, start)
    return (start.astype(jnp.int32), (start + length).astype(jnp.int32))


def draw_span_start(key, part):
    return span_pair(key)[0]


def draw_span_end(key, part):
    return span_pair(key)[1]


def level_of(stream_key, shape, shards, least, high):
    def one(position, parts):
        heights = jax.random.uniform(jax.random.fold_in(jax.random.fold_in(stream_key, 6), position), (parts,), jnp.float32, least / len(shards), high / len(shards))
        return jnp.repeat(jnp.exp(heights), shape[position] // parts).reshape((-1,) + (1,) * (len(shape) - position - 1))

    level = one(*shards[0])
    for cut in shards[1:]:
        level = level * one(*cut)
    return level


def split_up(count, total, bound, slope):
    loads = [(1 << 20) // math.isqrt(grade ** slope) + 1 for grade in range(2, count + 1)]
    rest, counts = total - bound - (count - 1), [1] * (count - 1)
    while rest > 0:
        candidates = [i for i in range(count - 1) if counts[i] < bound]
        mass, remaining = sum([loads[i] for i in candidates]), rest
        for i in candidates:
            addition = min(bound - counts[i], max(1, remaining * loads[i] // mass), rest)
            counts[i] = counts[i] + addition
            rest = rest - addition
    return np.array([bound] + counts)


def ragged_sizes(stream_key, amount, total, most, slope):
    if amount == 2:
        one = jax.random.randint(stream_key, (), max(1, total - most), min(most, total - 1) + 1)
        return jnp.stack([one, total - one])
    lengths = jnp.asarray(split_up(amount, total, most, slope), jnp.int32)
    twos = (amount - 1) // 2
    donor, receiver = lengths[1:1 + 2 * twos:2], lengths[2:2 + 2 * twos:2]
    room = jnp.minimum(donor - 1, most - receiver)
    moved = jax.random.randint(jax.random.fold_in(stream_key, 1), (twos,), 0, 1 << 20) % (room + 1)
    lengths = lengths.at[1:1 + 2 * twos:2].set(donor - moved).at[2:2 + 2 * twos:2].set(receiver + moved)
    return lengths[jax.random.permutation(jax.random.fold_in(stream_key, 2), amount)]


def scatter_about(stream_key, shape, scale, bound, cuts=(), held_as=jnp.bfloat16):
    entries = jax.random.normal(stream_key, shape, jnp.float32) * scale
    if len(cuts) > 0:
        entries = level_of(stream_key, shape, cuts, -0.22, 0.18) * entries
    return jnp.clip(entries, min=-bound, max=bound).astype(held_as)


def setup_inputs(seed: int = 0) -> dict:
    key_list = jax.random.split(jax.random.key(seed), 8)
    return {
        "queries": draw_queries(jax.random.fold_in(key_list[7], 71), 0),
        "keys": draw_keys(jax.random.fold_in(key_list[7], 71), 0),
        "values": scatter_about(key_list[2], (SEQ, HEADS * HEAD_DIM), 1.0, 6.0, ((0, 32), (1, 4))),
        "doc_ids": jnp.searchsorted(jnp.cumsum(ragged_sizes(key_list[3], NDOC, NB, DOC_MOST, 2)), jnp.arange(NB), side="right").astype(jnp.int32),
        "span_start": draw_span_start(jax.random.fold_in(key_list[7], 71), 0),
        "span_end": draw_span_end(jax.random.fold_in(key_list[7], 71), 0),
        "out_weight": scatter_about(key_list[6], (HEADS * HEAD_DIM, D), (HEADS * HEAD_DIM) ** -0.5, 0.125, ((0, 4),)),
    }


NEG = -1e+30

def block_spans(span_start, span_end, count):
    blocks = jnp.arange(count, dtype=jnp.int32)
    inside = (blocks[:, None] >= span_start[None, :]) & (blocks[:, None] < span_end[None, :])
    labels = jnp.arange(1, span_start.shape[0] + 1, dtype=jnp.int32)
    return lax.optimization_barrier(jnp.sum(jnp.where(inside, labels[None, :], 0), axis=1)).astype(jnp.int32) - 1

def reference(queries, keys, values, doc_ids, span_start, span_end, out_weight):
    seq_len = queries.shape[0]
    block_count = seq_len // BLOCK
    span_blocks = block_spans(span_start, span_end, block_count)
    positions = jnp.arange(seq_len, dtype=jnp.int32)
    doc_tok = doc_ids[positions // BLOCK]
    span_tok = span_blocks[positions // BLOCK]
    key_heads = keys.astype(jnp.float32).reshape(seq_len, HEADS, HEAD_DIM)
    value_heads = values.astype(jnp.float32).reshape(seq_len, HEADS, HEAD_DIM)
    scale = 1.0 / math.sqrt(HEAD_DIM)

    def one_block(index):
        first = (index * BLOCK).astype(jnp.int32)
        query_heads = lax.dynamic_slice_in_dim(queries, first, BLOCK, 0).astype(jnp.float32).reshape(BLOCK, HEADS, HEAD_DIM)
        query_pos = first + jnp.arange(BLOCK, dtype=jnp.int32)
        query_doc = lax.dynamic_slice_in_dim(doc_tok, first, BLOCK, 0)
        query_span = lax.dynamic_slice_in_dim(span_tok, first, BLOCK, 0)
        allowed = (query_doc[:, None] == doc_tok[None, :]) & ((positions[None, :] <= query_pos[:, None]) | (query_span[:, None] == span_tok[None, :]) & (query_span[:, None] >= 0))
        scores = jnp.einsum('qhd,khd->hqk', query_heads, key_heads) * scale
        scores = jnp.where(allowed[None], scores, NEG)
        row_max = lax.optimization_barrier(jnp.max(scores, axis=2, keepdims=True))
        weights = jnp.where(allowed[None], jnp.exp(scores - row_max), 0.0)
        totals = lax.optimization_barrier(jnp.sum(weights, axis=2))
        rounded = lax.optimization_barrier(weights.astype(jnp.bfloat16)).astype(jnp.float32)
        attended = jnp.einsum('hqk,khd->qhd', rounded, value_heads) / totals.T[:, :, None]
        return attended.reshape(BLOCK, HEADS * HEAD_DIM).astype(jnp.bfloat16)
    attended = lax.map(one_block, jnp.arange(block_count, dtype=jnp.int32)).reshape(seq_len, HEADS * HEAD_DIM)
    return jnp.dot(attended, out_weight, preferred_element_type=jnp.float32).astype(jnp.bfloat16)
```

```python
import math

import jax
import jax.numpy as jnp
import numpy as np
from jax import lax
from jax.experimental import pallas as pl
from jax.experimental.pallas import tpu as pltpu
from jax.sharding import Mesh, NamedSharding, PartitionSpec as P

HEAD_DIM = 128
BLOCK = 128
DOC_MOST = 80
SPAN_MOST = 4
TQ = 512
TK = 512

NEG = -1e30


def block_spans(span_start, span_end, count):
    blocks = jnp.arange(count, dtype=jnp.int32)
    inside = (blocks[:, None] >= span_start[None, :]) & (blocks[:, None] < span_end[None, :])
    labels = jnp.arange(1, span_start.shape[0] + 1, dtype=jnp.int32)
    return jnp.sum(jnp.where(inside, labels[None, :], 0), axis=1) - 1


def attention_kernel(lo_ref, cnt_ref, qoff_ref, q_ref, k_ref, v_ref, qd_ref, qs_ref, kd_ref, ks_ref,
                     o_ref, m_sc, l_sc, acc_sc):
    qi = pl.program_id(0)
    step = pl.program_id(1)
    scale = 1.0 / math.sqrt(HEAD_DIM)

    @pl.when(step == 0)
    def _():
        m_sc[...] = jnp.full(m_sc.shape, NEG, jnp.float32)
        l_sc[...] = jnp.zeros(l_sc.shape, jnp.float32)
        acc_sc[...] = jnp.zeros(acc_sc.shape, jnp.float32)

    @pl.when(step < cnt_ref[qi])
    def _():
        kt = lo_ref[qi] + step
        scores = lax.dot_general(
            q_ref[...], k_ref[...], (((1,), (1,)), ((), ())), preferred_element_type=jnp.float32
        ) * scale
        qpos = qoff_ref[0] + qi * TQ + lax.broadcasted_iota(jnp.int32, (TQ, TK), 0)
        kpos = kt * TK + lax.broadcasted_iota(jnp.int32, (TQ, TK), 1)
        allowed = (qd_ref[...] == kd_ref[...]) & ((kpos <= qpos) | (qs_ref[...] == ks_ref[...]))
        scores = jnp.where(allowed, scores, NEG)
        m_old = m_sc[...]
        m_new = jnp.maximum(m_old, jnp.max(scores, axis=1, keepdims=True))
        weights = jnp.where(allowed, jnp.exp(scores - m_new), 0.0)
        factor = jnp.exp(m_old - m_new)
        l_sc[...] = l_sc[...] * factor + jnp.sum(weights, axis=1, keepdims=True)
        acc_sc[...] = acc_sc[...] * factor + jnp.dot(
            weights.astype(jnp.bfloat16), v_ref[...], preferred_element_type=jnp.float32
        )
        m_sc[...] = m_new

    @pl.when(step == pl.num_programs(1) - 1)
    def _():
        o_ref[...] = (acc_sc[...] / l_sc[...]).astype(o_ref.dtype)


def attend_head(lo, cnt, qoff, q, k, v, qd, qs, kd, ks, steps):
    nq = q.shape[0] // TQ

    def kmap(i, s, lo_ref, cnt_ref, qoff_ref):
        return (lo_ref[i] + jnp.minimum(s, cnt_ref[i] - 1), 0)

    def klab(i, s, lo_ref, cnt_ref, qoff_ref):
        return (0, lo_ref[i] + jnp.minimum(s, cnt_ref[i] - 1))

    def qmap(i, s, *_):
        return (i, 0)

    grid_spec = pltpu.PrefetchScalarGridSpec(
        num_scalar_prefetch=3,
        grid=(nq, steps),
        in_specs=[
            pl.BlockSpec((TQ, HEAD_DIM), qmap),
            pl.BlockSpec((TK, HEAD_DIM), kmap),
            pl.BlockSpec((TK, HEAD_DIM), kmap),
            pl.BlockSpec((TQ, 1), qmap),
            pl.BlockSpec((TQ, 1), qmap),
            pl.BlockSpec((1, TK), klab),
            pl.BlockSpec((1, TK), klab),
        ],
        out_specs=pl.BlockSpec((TQ, HEAD_DIM), qmap),
        scratch_shapes=[
            pltpu.VMEM((TQ, 1), jnp.float32),
            pltpu.VMEM((TQ, 1), jnp.float32),
            pltpu.VMEM((TQ, HEAD_DIM), jnp.float32),
        ],
    )
    return pl.pallas_call(
        attention_kernel,
        out_shape=jax.ShapeDtypeStruct(q.shape, jnp.bfloat16),
        grid_spec=grid_spec,
        compiler_params=pltpu.CompilerParams(dimension_semantics=("arbitrary", "arbitrary")),
    )(lo, cnt, qoff, q, k, v, qd, qs, kd, ks)


def tile_ranges(doc_ids, span_blocks, span_end, qfirst, nq, ntk):
    count = doc_ids.shape[0]
    blocks = jnp.arange(count, dtype=jnp.int32)
    same = doc_ids[:, None] == doc_ids[None, :]
    doc_lo = jnp.min(jnp.where(same, blocks[None, :], count), axis=1)
    doc_hi = jnp.max(jnp.where(same, blocks[None, :], -1), axis=1)
    span_hi = jnp.where(span_blocks >= 0, span_end[jnp.maximum(span_blocks, 0)] - 1, blocks)
    key_hi = jnp.minimum(jnp.maximum(span_hi, blocks), doc_hi)
    per_tile = TQ // BLOCK
    qblocks = qfirst // BLOCK + jnp.arange(nq * per_tile, dtype=jnp.int32)
    lo_blk = jnp.min(doc_lo[qblocks].reshape(nq, per_tile), axis=1)
    hi_blk = jnp.max(key_hi[qblocks].reshape(nq, per_tile), axis=1)
    lo_t = lo_blk * BLOCK // TK
    hi_t = hi_blk * BLOCK // TK
    return lo_t.astype(jnp.int32), (hi_t - lo_t + 1).astype(jnp.int32)


def per_device(queries, keys, values, doc_ids, span_start, span_end, out_weight):
    rows, local_width = queries.shape
    group = lax.axis_size("cl")
    chunk = rows * group
    cg = lax.axis_index("cg")

    def to_heads(x):
        return lax.all_to_all(x, "cl", 1, 0, tiled=True)

    q1 = to_heads(queries)
    k1 = to_heads(keys)
    v1 = to_heads(values)
    k_all = lax.all_gather(k1, "cg", axis=0, tiled=True)
    v_all = lax.all_gather(v1, "cg", axis=0, tiled=True)
    seq = k_all.shape[0]

    count = doc_ids.shape[0]
    span_blocks = block_spans(span_start, span_end, count)
    positions = jnp.arange(seq, dtype=jnp.int32)
    doc_tok = doc_ids[positions // BLOCK]
    span_tok = span_blocks[positions // BLOCK]
    key_span = jnp.where(span_tok >= 0, span_tok, -2)
    query_span = jnp.where(span_tok >= 0, span_tok, -1)
    qfirst = cg * chunk
    qd = lax.dynamic_slice_in_dim(doc_tok, qfirst, chunk).reshape(chunk, 1)
    qs = lax.dynamic_slice_in_dim(query_span, qfirst, chunk).reshape(chunk, 1)
    kd = doc_tok.reshape(1, seq)
    ks = key_span.reshape(1, seq)

    nq = chunk // TQ
    ntk = seq // TK
    lo, cnt = tile_ranges(doc_ids, span_blocks, span_end, qfirst, nq, ntk)
    window = (DOC_MOST - 1) + TQ // BLOCK + (SPAN_MOST - 1)
    steps = min(ntk, (window - 1) // (TK // BLOCK) + 2)
    cnt = jnp.clip(cnt, 1, steps)
    qoff = jnp.reshape(qfirst, (1,)).astype(jnp.int32)

    att1 = attend_head(lo, cnt, qoff, q1, k_all, v_all, qd, qs, kd, ks, steps)
    attended = lax.all_to_all(att1, "cl", 0, 1, tiled=True)
    mixed = lax.psum_scatter(
        jnp.dot(attended, out_weight, preferred_element_type=jnp.float32).astype(jnp.bfloat16),
        "tp",
        scatter_dimension=0,
        tiled=True,
    )
    return mixed


def solution(mesh):
    n_ctx = mesh.shape["ctx"]
    n_tp = mesh.shape["tp"]
    group = 4
    inner = Mesh(np.asarray(mesh.devices).reshape(n_ctx // group, group, n_tp), ("cg", "cl", "tp"))
    out_sharding = NamedSharding(mesh, P(("ctx", "tp"), None))
    body = jax.shard_map(
        per_device,
        mesh=inner,
        in_specs=(
            P(("cg", "cl"), "tp"),
            P(("cg", "cl"), "tp"),
            P(("cg", "cl"), "tp"),
            P(),
            P(),
            P(),
            P("tp", None),
        ),
        out_specs=P(("cg", "cl", "tp"), None),
        check_vma=False,
    )

    def run(*args):
        return lax.with_sharding_constraint(body(*args), out_sharding)

    return run
```

```python
import math

import jax
import jax.numpy as jnp
import numpy as np
from jax import lax
from jax.experimental import pallas as pl
from jax.experimental.pallas import tpu as pltpu
from jax.sharding import Mesh, NamedSharding, PartitionSpec as P

HEAD_DIM = 128
BLOCK = 128
DOC_MOST = 80
SPAN_MOST = 4
TK = 512

NEG = -1e30


def block_spans(span_start, span_end, count):
    blocks = jnp.arange(count, dtype=jnp.int32)
    inside = (blocks[:, None] >= span_start[None, :]) & (blocks[:, None] < span_end[None, :])
    labels = jnp.arange(1, span_start.shape[0] + 1, dtype=jnp.int32)
    return jnp.sum(jnp.where(inside, labels[None, :], 0), axis=1) - 1


def make_kernel(tq):
    scale = 1.0 / math.sqrt(HEAD_DIM)

    def kernel(qt_ref, kt_ref, first_ref, last_ref, mode_ref, qstart_ref,
               q_ref, k_ref, v_ref, qd_ref, qs_ref, kd_ref, ks_ref, o_ref, m_sc, l_sc, acc_sc):
        p = pl.program_id(0)
        mode = mode_ref[p]

        @pl.when(first_ref[p] == 1)
        def _():
            m_sc[...] = jnp.full(m_sc.shape, NEG, jnp.float32)
            l_sc[...] = jnp.zeros(l_sc.shape, jnp.float32)
            acc_sc[...] = jnp.zeros(acc_sc.shape, jnp.float32)

        def update(masked):
            scores = lax.dot_general(
                q_ref[...], k_ref[...], (((1,), (1,)), ((), ())), preferred_element_type=jnp.float32
            ) * scale
            m_old = m_sc[...]
            if masked:
                qpos = qstart_ref[qt_ref[p]] + lax.broadcasted_iota(jnp.int32, (tq, TK), 0)
                kpos = kt_ref[p] * TK + lax.broadcasted_iota(jnp.int32, (tq, TK), 1)
                allowed = (qd_ref[...] == kd_ref[...]) & ((kpos <= qpos) | (qs_ref[...] == ks_ref[...]))
                scores = jnp.where(allowed, scores, NEG)
                m_new = jnp.maximum(m_old, jnp.max(scores, axis=1, keepdims=True))
                weights = jnp.where(allowed, jnp.exp(scores - m_new), 0.0)
            else:
                m_new = jnp.maximum(m_old, jnp.max(scores, axis=1, keepdims=True))
                weights = jnp.exp(scores - m_new)
            factor = jnp.exp(m_old - m_new)
            l_sc[...] = l_sc[...] * factor + jnp.sum(weights, axis=1, keepdims=True)
            acc_sc[...] = acc_sc[...] * factor + jnp.dot(
                weights.astype(jnp.bfloat16), v_ref[...], preferred_element_type=jnp.float32
            )
            m_sc[...] = m_new

        @pl.when(mode == 1)
        def _():
            update(True)

        @pl.when(mode == 2)
        def _():
            update(False)

        @pl.when(last_ref[p] == 1)
        def _():
            o_ref[...] = (acc_sc[...] / l_sc[...]).astype(o_ref.dtype)

    return kernel


def attend_head(tables, q, kv, qd, qs, kd, ks, tq):
    total = tables[0].shape[0]

    def qmap(p, qt, kt, *_):
        return (qt[p], 0)

    def kmap(p, qt, kt, *_):
        return (kt[p], 0)

    def vmap(p, qt, kt, *_):
        return (kt[p], 1)

    def klab(p, qt, kt, *_):
        return (0, kt[p])

    grid_spec = pltpu.PrefetchScalarGridSpec(
        num_scalar_prefetch=len(tables),
        grid=(total,),
        in_specs=[
            pl.BlockSpec((tq, HEAD_DIM), qmap),
            pl.BlockSpec((TK, HEAD_DIM), kmap),
            pl.BlockSpec((TK, HEAD_DIM), vmap),
            pl.BlockSpec((tq, 1), qmap),
            pl.BlockSpec((tq, 1), qmap),
            pl.BlockSpec((1, TK), klab),
            pl.BlockSpec((1, TK), klab),
        ],
        out_specs=pl.BlockSpec((tq, HEAD_DIM), qmap),
        scratch_shapes=[
            pltpu.VMEM((tq, 1), jnp.float32),
            pltpu.VMEM((tq, 1), jnp.float32),
            pltpu.VMEM((tq, HEAD_DIM), jnp.float32),
        ],
    )
    return pl.pallas_call(
        make_kernel(tq),
        out_shape=jax.ShapeDtypeStruct(q.shape, jnp.bfloat16),
        grid_spec=grid_spec,
        compiler_params=pltpu.CompilerParams(dimension_semantics=("arbitrary",)),
    )(*tables, q, kv, kv, qd, qs, kd, ks)


def take(table, index):
    slots = jnp.arange(table.shape[0], dtype=jnp.int32)
    return jnp.sum(jnp.where(index[..., None] == slots, table, 0), axis=-1)


def step_tables(doc_ids, span_blocks, span_end, qstart, tq, seq):
    count = doc_ids.shape[0]
    nq = qstart.shape[0]
    per_q = tq // BLOCK
    per_k = TK // BLOCK
    ntk = seq // TK
    blocks = jnp.arange(count, dtype=jnp.int32)
    same = doc_ids[:, None] == doc_ids[None, :]
    doc_lo = jnp.min(jnp.where(same, blocks[None, :], count), axis=1)
    doc_hi = jnp.max(jnp.where(same, blocks[None, :], -1), axis=1)
    span_hi = jnp.where(span_blocks >= 0, take(span_end, span_blocks) - 1, blocks)
    key_hi = jnp.minimum(jnp.maximum(span_hi, blocks), doc_hi)
    qblocks = (qstart // BLOCK)[:, None] + jnp.arange(per_q, dtype=jnp.int32)[None, :]
    lo_t = jnp.min(take(doc_lo, qblocks), axis=1) // per_k
    hi_t = jnp.max(take(key_hi, qblocks), axis=1) // per_k
    window = (DOC_MOST - 1) + per_q + (SPAN_MOST - 1)
    most = min(ntk, (window - 1) // per_k + 2)
    cnt = jnp.clip(hi_t - lo_t + 1, 1, most)
    ends = jnp.cumsum(cnt)
    starts = ends - cnt
    total = nq * most
    pos = jnp.arange(total, dtype=jnp.int32)
    qt = jnp.minimum(jnp.sum((pos[:, None] >= ends[None, :]).astype(jnp.int32), axis=1), nq - 1)
    live = pos < ends[-1]
    local = jnp.where(live, pos - take(starts, qt), take(cnt, qt) - 1)
    kt = take(lo_t, qt) + local
    first = (live & (local == 0)).astype(jnp.int32)
    last = (live & (local == take(cnt, qt) - 1)).astype(jnp.int32)
    qdoc = take(doc_ids, qblocks)
    kblocks = kt[:, None] * per_k + jnp.arange(per_k, dtype=jnp.int32)[None, :]
    kdoc = take(doc_ids, kblocks)
    qdoc_t = jnp.sum(jnp.where((qt[:, None] == jnp.arange(nq))[:, :, None], qdoc[None], 0), axis=1)
    one_doc = (jnp.min(qdoc_t, axis=1) == jnp.max(qdoc_t, axis=1)) & (
        jnp.min(kdoc, axis=1) == jnp.max(kdoc, axis=1)) & (qdoc_t[:, 0] == kdoc[:, 0])
    below = (kt + 1) * TK - 1 <= take(qstart, qt)
    mode = jnp.where(live, jnp.where(one_doc & below, 2, 1), 0).astype(jnp.int32)
    return (qt.astype(jnp.int32), kt.astype(jnp.int32), first, last, mode, qstart.astype(jnp.int32))


def per_device(queries, keys, values, doc_ids, span_start, span_end, out_weight):
    rows, local_width = queries.shape
    group = lax.axis_size("cl")
    n_cg = lax.axis_size("cg")
    chunk = rows * group
    piece = chunk // n_cg
    j = lax.axis_index("cg")

    stacked = lax.all_to_all(jnp.stack([queries, keys, values]), "cl", 2, 1, tiled=True)
    q1 = lax.all_to_all(stacked[0], "cg", 0, 0, tiled=True)
    kv1 = jnp.concatenate([stacked[1], stacked[2]], axis=1)
    kv_all = lax.all_gather(kv1, "cg", axis=0, tiled=True)
    seq = kv_all.shape[0]

    count = doc_ids.shape[0]
    span_blocks = block_spans(span_start, span_end, count)
    doc_tok = jnp.broadcast_to(doc_ids[:, None], (count, BLOCK)).reshape(seq)
    span_tok = jnp.broadcast_to(span_blocks[:, None], (count, BLOCK)).reshape(seq)
    key_span = jnp.where(span_tok >= 0, span_tok, -2)
    query_span = jnp.where(span_tok >= 0, span_tok, -1)

    def mine(x):
        return lax.dynamic_index_in_dim(x.reshape(n_cg, n_cg, piece), j, axis=1, keepdims=False).reshape(
            chunk, 1)

    qd = mine(doc_tok)
    qs = mine(query_span)
    kd = doc_tok.reshape(1, seq)
    ks = key_span.reshape(1, seq)
    qstart = jnp.arange(n_cg, dtype=jnp.int32) * chunk + j * piece

    tables = step_tables(doc_ids, span_blocks, span_end, qstart, piece, seq)
    att1 = attend_head(tables, q1, kv_all, qd, qs, kd, ks, piece)
    att0 = lax.all_to_all(att1, "cg", 0, 0, tiled=True)
    attended = lax.all_to_all(att0, "cl", 0, 1, tiled=True)
    mixed = lax.psum_scatter(
        jnp.dot(attended, out_weight, preferred_element_type=jnp.float32).astype(jnp.bfloat16),
        "tp",
        scatter_dimension=0,
        tiled=True,
    )
    return mixed


def solution(mesh):
    n_ctx = mesh.shape["ctx"]
    n_tp = mesh.shape["tp"]
    group = 4
    inner = Mesh(np.asarray(mesh.devices).reshape(n_ctx // group, group, n_tp), ("cg", "cl", "tp"))
    out_sharding = NamedSharding(mesh, P(("ctx", "tp"), None))
    body = jax.shard_map(
        per_device,
        mesh=inner,
        in_specs=(
            P(("cg", "cl"), "tp"),
            P(("cg", "cl"), "tp"),
            P(("cg", "cl"), "tp"),
            P(),
            P(),
            P(),
            P("tp", None),
        ),
        out_specs=P(("cg", "cl", "tp"), None),
        check_vma=False,
    )

    def run(*args):
        return lax.with_sharding_constraint(body(*args), out_sharding)

    return run
```

```python
import math

import jax
import jax.numpy as jnp
import numpy as np
from jax import lax
from jax.experimental import pallas as pl
from jax.experimental.pallas import tpu as pltpu
from jax.sharding import Mesh, NamedSharding, PartitionSpec as P

HEAD_DIM = 128
BLOCK = 128
DOC_MOST = 80
SPAN_MOST = 4
TK = 512

NEG = -1e30


def block_spans(span_start, span_end, count):
    blocks = jnp.arange(count, dtype=jnp.int32)
    inside = (blocks[:, None] >= span_start[None, :]) & (blocks[:, None] < span_end[None, :])
    labels = jnp.arange(1, span_start.shape[0] + 1, dtype=jnp.int32)
    return jnp.sum(jnp.where(inside, labels[None, :], 0), axis=1) - 1


def make_kernel(tq):
    scale = 1.0 / math.sqrt(HEAD_DIM)

    def kernel(qt_ref, kt_ref, first_ref, last_ref, mode_ref, qstart_ref,
               q_ref, k_ref, v_ref, qd_ref, qs_ref, kd_ref, ks_ref, o_ref, m_sc, l_sc, acc_sc):
        p = pl.program_id(0)
        mode = mode_ref[p]

        @pl.when(first_ref[p] == 1)
        def _():
            m_sc[...] = jnp.full(m_sc.shape, NEG, jnp.float32)
            l_sc[...] = jnp.zeros(l_sc.shape, jnp.float32)
            acc_sc[...] = jnp.zeros(acc_sc.shape, jnp.float32)

        def update(masked):
            scores = lax.dot_general(
                q_ref[...], k_ref[...], (((1,), (1,)), ((), ())), preferred_element_type=jnp.float32
            ) * scale
            m_old = m_sc[...]
            if masked:
                qpos = qstart_ref[qt_ref[p]] + lax.broadcasted_iota(jnp.int32, (tq, TK), 0)
                kpos = kt_ref[p] * TK + lax.broadcasted_iota(jnp.int32, (tq, TK), 1)
                allowed = (qd_ref[...] == kd_ref[...]) & ((kpos <= qpos) | (qs_ref[...] == ks_ref[...]))
                scores = jnp.where(allowed, scores, NEG)
                m_new = jnp.maximum(m_old, jnp.max(scores, axis=1, keepdims=True))
                weights = jnp.where(allowed, jnp.exp(scores - m_new), 0.0)
            else:
                m_new = jnp.maximum(m_old, jnp.max(scores, axis=1, keepdims=True))
                weights = jnp.exp(scores - m_new)
            factor = jnp.exp(m_old - m_new)
            l_sc[...] = l_sc[...] * factor + jnp.sum(weights, axis=1, keepdims=True)
            acc_sc[...] = acc_sc[...] * factor + jnp.dot(
                weights.astype(jnp.bfloat16), v_ref[...], preferred_element_type=jnp.float32
            )
            m_sc[...] = m_new

        @pl.when(mode == 1)
        def _():
            update(True)

        @pl.when(mode == 2)
        def _():
            update(False)

        @pl.when(last_ref[p] == 1)
        def _():
            o_ref[...] = (acc_sc[...] / l_sc[...]).astype(o_ref.dtype)

    return kernel


def attend_head(tables, q, kv, qd, qs, kd, ks, tq):
    total = tables[0].shape[0]

    def qmap(p, qt, kt, *_):
        return (qt[p], 0)

    def kmap(p, qt, kt, *_):
        return (kt[p], 0)

    def vmap(p, qt, kt, *_):
        return (kt[p], 1)

    def klab(p, qt, kt, *_):
        return (0, kt[p])

    grid_spec = pltpu.PrefetchScalarGridSpec(
        num_scalar_prefetch=len(tables),
        grid=(total,),
        in_specs=[
            pl.BlockSpec((tq, HEAD_DIM), qmap),
            pl.BlockSpec((TK, HEAD_DIM), kmap),
            pl.BlockSpec((TK, HEAD_DIM), vmap),
            pl.BlockSpec((tq, 1), qmap),
            pl.BlockSpec((tq, 1), qmap),
            pl.BlockSpec((1, TK), klab),
            pl.BlockSpec((1, TK), klab),
        ],
        out_specs=pl.BlockSpec((tq, HEAD_DIM), qmap),
        scratch_shapes=[
            pltpu.VMEM((tq, 1), jnp.float32),
            pltpu.VMEM((tq, 1), jnp.float32),
            pltpu.VMEM((tq, HEAD_DIM), jnp.float32),
        ],
    )
    return pl.pallas_call(
        make_kernel(tq),
        out_shape=jax.ShapeDtypeStruct(q.shape, jnp.bfloat16),
        grid_spec=grid_spec,
        compiler_params=pltpu.CompilerParams(dimension_semantics=("arbitrary",)),
    )(*tables, q, kv, kv, qd, qs, kd, ks)


def take(table, index):
    slots = jnp.arange(table.shape[0], dtype=jnp.int32)
    return jnp.sum(jnp.where(index[..., None] == slots, table, 0), axis=-1)


def step_tables(doc_ids, span_blocks, span_end, qstart, tq, seq):
    count = doc_ids.shape[0]
    nq = qstart.shape[0]
    per_q = tq // BLOCK
    per_k = TK // BLOCK
    ntk = seq // TK
    blocks = jnp.arange(count, dtype=jnp.int32)
    same = doc_ids[:, None] == doc_ids[None, :]
    doc_lo = jnp.min(jnp.where(same, blocks[None, :], count), axis=1)
    doc_hi = jnp.max(jnp.where(same, blocks[None, :], -1), axis=1)
    span_hi = jnp.where(span_blocks >= 0, take(span_end, span_blocks) - 1, blocks)
    key_hi = jnp.minimum(jnp.maximum(span_hi, blocks), doc_hi)
    qblocks = (qstart // BLOCK)[:, None] + jnp.arange(per_q, dtype=jnp.int32)[None, :]
    lo_t = jnp.min(take(doc_lo, qblocks), axis=1) // per_k
    hi_t = jnp.max(take(key_hi, qblocks), axis=1) // per_k
    window = (DOC_MOST - 1) + per_q + (SPAN_MOST - 1)
    most = min(ntk, (window - 1) // per_k + 2)
    cnt = jnp.clip(hi_t - lo_t + 1, 1, most)
    ends = jnp.cumsum(cnt)
    starts = ends - cnt
    total = nq * most
    pos = jnp.arange(total, dtype=jnp.int32)
    qt = jnp.minimum(jnp.sum((pos[:, None] >= ends[None, :]).astype(jnp.int32), axis=1), nq - 1)
    live = pos < ends[-1]
    local = jnp.where(live, pos - take(starts, qt), take(cnt, qt) - 1)
    kt = take(lo_t, qt) + local
    first = (live & (local == 0)).astype(jnp.int32)
    last = (live & (local == take(cnt, qt) - 1)).astype(jnp.int32)
    qdoc = take(doc_ids, qblocks)
    kblocks = kt[:, None] * per_k + jnp.arange(per_k, dtype=jnp.int32)[None, :]
    kdoc = take(doc_ids, kblocks)
    qdoc_t = jnp.sum(jnp.where((qt[:, None] == jnp.arange(nq))[:, :, None], qdoc[None], 0), axis=1)
    one_doc = (jnp.min(qdoc_t, axis=1) == jnp.max(qdoc_t, axis=1)) & (
        jnp.min(kdoc, axis=1) == jnp.max(kdoc, axis=1)) & (qdoc_t[:, 0] == kdoc[:, 0])
    below = (kt + 1) * TK - 1 <= take(qstart, qt)
    mode = jnp.where(live, jnp.where(one_doc & below, 2, 1), 0).astype(jnp.int32)
    return (qt.astype(jnp.int32), kt.astype(jnp.int32), first, last, mode, qstart.astype(jnp.int32))


def shifted(x, axis, s):
    n = lax.axis_size(axis)
    return lax.ppermute(x, axis, [(i, (i + s) % n) for i in range(n)])


def exchange(x, axis, split_axis, concat_axis):
    n = lax.axis_size(axis)
    me = lax.axis_index(axis)
    size = x.shape[split_axis] // n
    out_shape = list(x.shape)
    out_shape[split_axis] = size
    out_shape[concat_axis] = out_shape[concat_axis] * n if split_axis != concat_axis else size * n
    width = x.shape[concat_axis] if split_axis != concat_axis else size
    out = jnp.zeros(out_shape, x.dtype)
    for s in range(n):
        part = lax.dynamic_slice_in_dim(x, ((me + s) % n) * size, size, split_axis)
        got = part if s == 0 else shifted(part, axis, s)
        out = lax.dynamic_update_slice_in_dim(out, got, ((me - s) % n) * width, concat_axis)
    return out


def gathered(x, axis):
    n = lax.axis_size(axis)
    me = lax.axis_index(axis)
    size = x.shape[0]
    out = jnp.zeros((size * n,) + x.shape[1:], x.dtype)
    for s in range(n):
        got = x if s == 0 else shifted(x, axis, s)
        out = lax.dynamic_update_slice_in_dim(out, got, ((me - s) % n) * size, 0)
    return out


def per_device(queries, keys, values, doc_ids, span_start, span_end, out_weight):
    rows, local_width = queries.shape
    group = lax.axis_size("cl")
    n_cg = lax.axis_size("cg")
    chunk = rows * group
    piece = chunk // n_cg
    j = lax.axis_index("cg")

    stacked = exchange(jnp.stack([queries, keys, values]), "cl", 2, 1)
    q1 = exchange(stacked[0], "cg", 0, 0)
    kv1 = jnp.concatenate([stacked[1], stacked[2]], axis=1)
    kv_all = gathered(kv1, "cg")
    seq = kv_all.shape[0]

    count = doc_ids.shape[0]
    span_blocks = block_spans(span_start, span_end, count)
    doc_tok = jnp.broadcast_to(doc_ids[:, None], (count, BLOCK)).reshape(seq)
    span_tok = jnp.broadcast_to(span_blocks[:, None], (count, BLOCK)).reshape(seq)
    key_span = jnp.where(span_tok >= 0, span_tok, -2)
    query_span = jnp.where(span_tok >= 0, span_tok, -1)

    def mine(x):
        return lax.dynamic_index_in_dim(x.reshape(n_cg, n_cg, piece), j, axis=1, keepdims=False).reshape(
            chunk, 1)

    qd = mine(doc_tok)
    qs = mine(query_span)
    kd = doc_tok.reshape(1, seq)
    ks = key_span.reshape(1, seq)
    qstart = jnp.arange(n_cg, dtype=jnp.int32) * chunk + j * piece

    tables = step_tables(doc_ids, span_blocks, span_end, qstart, piece, seq)
    att1 = attend_head(tables, q1, kv_all, qd, qs, kd, ks, piece)
    att0 = exchange(att1, "cg", 0, 0)
    attended = exchange(att0, "cl", 0, 1)
    mixed = lax.psum_scatter(
        jnp.dot(attended, out_weight, preferred_element_type=jnp.float32).astype(jnp.bfloat16),
        "tp",
        scatter_dimension=0,
        tiled=True,
    )
    return mixed


def solution(mesh):
    n_ctx = mesh.shape["ctx"]
    n_tp = mesh.shape["tp"]
    group = 4
    inner = Mesh(np.asarray(mesh.devices).reshape(n_ctx // group, group, n_tp), ("cg", "cl", "tp"))
    out_sharding = NamedSharding(mesh, P(("ctx", "tp"), None))
    body = jax.shard_map(
        per_device,
        mesh=inner,
        in_specs=(
            P(("cg", "cl"), "tp"),
            P(("cg", "cl"), "tp"),
            P(("cg", "cl"), "tp"),
            P(),
            P(),
            P(),
            P("tp", None),
        ),
        out_specs=P(("cg", "cl", "tp"), None),
        check_vma=False,
    )

    def run(*args):
        return lax.with_sharding_constraint(body(*args), out_sharding)

    return run
```

```python
import math

import jax
import jax.numpy as jnp
import numpy as np
from jax import lax
from jax.experimental import pallas as pl
from jax.experimental.pallas import tpu as pltpu
from jax.sharding import Mesh, NamedSharding, PartitionSpec as P

HEAD_DIM = 128
BLOCK = 128
DOC_MOST = 80
SPAN_MOST = 4
TK = 512

NEG = -1e30


def block_spans(span_start, span_end, count):
    blocks = jnp.arange(count, dtype=jnp.int32)
    inside = (blocks[:, None] >= span_start[None, :]) & (blocks[:, None] < span_end[None, :])
    labels = jnp.arange(1, span_start.shape[0] + 1, dtype=jnp.int32)
    return jnp.sum(jnp.where(inside, labels[None, :], 0), axis=1) - 1


def make_kernel(tq):
    scale = 1.0 / math.sqrt(HEAD_DIM)

    def kernel(qt_ref, kt_ref, kb_ref, first_ref, mode_ref, qstart_ref,
               q_ref, k_ref, v_ref, qd_ref, qs_ref, kd_ref, ks_ref, m_in, l_in, acc_in,
               m_sc, l_sc, acc_sc):
        p = pl.program_id(0)
        mode = mode_ref[p]

        @pl.when(first_ref[p] == 1)
        def _():
            m_sc[...] = m_in[...]
            l_sc[...] = l_in[...]
            acc_sc[...] = acc_in[...]

        def update(masked):
            scores = lax.dot_general(
                q_ref[...], k_ref[...], (((1,), (1,)), ((), ())), preferred_element_type=jnp.float32
            ) * scale
            m_old = m_sc[...]
            if masked:
                qpos = qstart_ref[qt_ref[p]] + lax.broadcasted_iota(jnp.int32, (tq, TK), 0)
                kpos = kt_ref[p] * TK + lax.broadcasted_iota(jnp.int32, (tq, TK), 1)
                allowed = (qd_ref[...] == kd_ref[...]) & ((kpos <= qpos) | (qs_ref[...] == ks_ref[...]))
                scores = jnp.where(allowed, scores, NEG)
                m_new = jnp.maximum(m_old, jnp.max(scores, axis=1, keepdims=True))
                weights = jnp.where(allowed, jnp.exp(scores - m_new), 0.0)
            else:
                m_new = jnp.maximum(m_old, jnp.max(scores, axis=1, keepdims=True))
                weights = jnp.exp(scores - m_new)
            factor = jnp.exp(m_old - m_new)
            l_sc[...] = l_sc[...] * factor + jnp.sum(weights, axis=1, keepdims=True)
            acc_sc[...] = acc_sc[...] * factor + jnp.dot(
                weights.astype(jnp.bfloat16), v_ref[...], preferred_element_type=jnp.float32
            )
            m_sc[...] = m_new

        @pl.when(mode == 1)
        def _():
            update(True)

        @pl.when(mode == 2)
        def _():
            update(False)

    return kernel


def attend_part(tables, q, kv, qd, qs, kd, ks, state, tq):
    total = tables[0].shape[0]

    def qmap(p, qt, *_):
        return (qt[p], 0)

    def kmap(p, qt, kt, kb, *_):
        return (kb[p], 0)

    def vmap(p, qt, kt, kb, *_):
        return (kb[p], 1)

    def klab(p, qt, kt, *_):
        return (0, kt[p])

    m, l, acc = state
    grid_spec = pltpu.PrefetchScalarGridSpec(
        num_scalar_prefetch=len(tables),
        grid=(total,),
        in_specs=[
            pl.BlockSpec((tq, HEAD_DIM), qmap),
            pl.BlockSpec((TK, HEAD_DIM), kmap),
            pl.BlockSpec((TK, HEAD_DIM), vmap),
            pl.BlockSpec((tq, 1), qmap),
            pl.BlockSpec((tq, 1), qmap),
            pl.BlockSpec((1, TK), klab),
            pl.BlockSpec((1, TK), klab),
            pl.BlockSpec((tq, 1), qmap),
            pl.BlockSpec((tq, 1), qmap),
            pl.BlockSpec((tq, HEAD_DIM), qmap),
        ],
        out_specs=[
            pl.BlockSpec((tq, 1), qmap),
            pl.BlockSpec((tq, 1), qmap),
            pl.BlockSpec((tq, HEAD_DIM), qmap),
        ],
    )
    n = len(tables)
    return pl.pallas_call(
        make_kernel(tq),
        out_shape=(
            jax.ShapeDtypeStruct(m.shape, jnp.float32),
            jax.ShapeDtypeStruct(l.shape, jnp.float32),
            jax.ShapeDtypeStruct(acc.shape, jnp.float32),
        ),
        grid_spec=grid_spec,
        input_output_aliases={n + 7: 0, n + 8: 1, n + 9: 2},
        compiler_params=pltpu.CompilerParams(dimension_semantics=("arbitrary",)),
    )(*tables, q, kv, kv, qd, qs, kd, ks, m, l, acc)


def take(table, index):
    slots = jnp.arange(table.shape[0], dtype=jnp.int32)
    return jnp.sum(jnp.where(index[..., None] == slots, table, 0), axis=-1)


def step_tables(doc_ids, span_blocks, span_end, qstart, tq, seq):
    count = doc_ids.shape[0]
    nq = qstart.shape[0]
    per_q = tq // BLOCK
    per_k = TK // BLOCK
    ntk = seq // TK
    blocks = jnp.arange(count, dtype=jnp.int32)
    same = doc_ids[:, None] == doc_ids[None, :]
    doc_lo = jnp.min(jnp.where(same, blocks[None, :], count), axis=1)
    doc_hi = jnp.max(jnp.where(same, blocks[None, :], -1), axis=1)
    span_hi = jnp.where(span_blocks >= 0, take(span_end, span_blocks) - 1, blocks)
    key_hi = jnp.minimum(jnp.maximum(span_hi, blocks), doc_hi)
    qblocks = (qstart // BLOCK)[:, None] + jnp.arange(per_q, dtype=jnp.int32)[None, :]
    lo_t = jnp.min(take(doc_lo, qblocks), axis=1) // per_k
    hi_t = jnp.max(take(key_hi, qblocks), axis=1) // per_k
    window = (DOC_MOST - 1) + per_q + (SPAN_MOST - 1)
    most = min(ntk, (window - 1) // per_k + 2)
    cnt = jnp.clip(hi_t - lo_t + 1, 1, most)
    ends = jnp.cumsum(cnt)
    starts = ends - cnt
    total = nq * most
    pos = jnp.arange(total, dtype=jnp.int32)
    qt = jnp.minimum(jnp.sum((pos[:, None] >= ends[None, :]).astype(jnp.int32), axis=1), nq - 1)
    live = pos < ends[-1]
    local = jnp.where(live, pos - take(starts, qt), take(cnt, qt) - 1)
    kt = take(lo_t, qt) + local
    first = (live & (local == 0)).astype(jnp.int32)
    last = (live & (local == take(cnt, qt) - 1)).astype(jnp.int32)
    qdoc = take(doc_ids, qblocks)
    kblocks = kt[:, None] * per_k + jnp.arange(per_k, dtype=jnp.int32)[None, :]
    kdoc = take(doc_ids, kblocks)
    qdoc_t = jnp.sum(jnp.where((qt[:, None] == jnp.arange(nq))[:, :, None], qdoc[None], 0), axis=1)
    one_doc = (jnp.min(qdoc_t, axis=1) == jnp.max(qdoc_t, axis=1)) & (
        jnp.min(kdoc, axis=1) == jnp.max(kdoc, axis=1)) & (qdoc_t[:, 0] == kdoc[:, 0])
    below = (kt + 1) * TK - 1 <= take(qstart, qt)
    mode = jnp.where(live, jnp.where(one_doc & below, 2, 1), 0).astype(jnp.int32)
    return qt.astype(jnp.int32), kt.astype(jnp.int32), mode, live, most


def part_tables(qt, kt, mode, live, part, parts, size, nq):
    total = qt.shape[0]
    pos = jnp.arange(total, dtype=jnp.int32)
    chosen = live & (kt % parts == part)
    n_sel = jnp.sum(chosen.astype(jnp.int32))
    order = jnp.argsort(jnp.where(chosen, pos, total + pos))[:size].astype(jnp.int32)
    i = jnp.arange(size, dtype=jnp.int32)
    keep = i < n_sel
    tail = take(order, jnp.maximum(n_sel - 1, 0)[None])[0]
    src = jnp.where(keep, order, tail)
    any_sel = n_sel > 0
    qt_p = jnp.where(any_sel, take(qt, src), nq - 1)
    kt_p = jnp.where(any_sel, take(kt, src), part)
    mode_p = jnp.where(keep, take(mode, src), 0)
    prev = jnp.concatenate([jnp.full((1,), -1, jnp.int32), qt_p[:-1]])
    first = ((i == 0) | (keep & (qt_p != prev))).astype(jnp.int32)
    return qt_p, kt_p, kt_p // parts, first, mode_p.astype(jnp.int32)


def per_device(queries, keys, values, doc_ids, span_start, span_end, out_weight):
    rows, local_width = queries.shape
    group = lax.axis_size("cl")
    n_cg = lax.axis_size("cg")
    chunk = rows * group
    piece = chunk // n_cg
    j = lax.axis_index("cg")

    stacked = lax.all_to_all(jnp.stack([queries, keys, values]), "cl", 2, 1, tiled=True)
    q1 = lax.all_to_all(stacked[0], "cg", 0, 0, tiled=True)
    kv1 = jnp.concatenate([stacked[1], stacked[2]], axis=1)
    parts = chunk // TK
    kv_parts = [lax.all_gather(kv1[p * TK:(p + 1) * TK], "cg", axis=0, tiled=True) for p in range(parts)]
    seq = chunk * n_cg

    count = doc_ids.shape[0]
    span_blocks = block_spans(span_start, span_end, count)
    doc_tok = jnp.broadcast_to(doc_ids[:, None], (count, BLOCK)).reshape(seq)
    span_tok = jnp.broadcast_to(span_blocks[:, None], (count, BLOCK)).reshape(seq)
    key_span = jnp.where(span_tok >= 0, span_tok, -2)
    query_span = jnp.where(span_tok >= 0, span_tok, -1)

    def mine(x):
        return lax.dynamic_index_in_dim(x.reshape(n_cg, n_cg, piece), j, axis=1, keepdims=False).reshape(
            chunk, 1)

    qd = mine(doc_tok)
    qs = mine(query_span)
    kd = doc_tok.reshape(1, seq)
    ks = key_span.reshape(1, seq)
    qstart = jnp.arange(n_cg, dtype=jnp.int32) * chunk + j * piece

    qt, kt, mode, live, most = step_tables(doc_ids, span_blocks, span_end, qstart, piece, seq)
    nq = n_cg
    size = nq * (-(-most // parts) + 1)
    state = (
        jnp.full((chunk, 1), NEG, jnp.float32),
        jnp.zeros((chunk, 1), jnp.float32),
        jnp.zeros((chunk, HEAD_DIM), jnp.float32),
    )
    for p in range(parts):
        qt_p, kt_p, kb_p, first_p, mode_p = part_tables(qt, kt, mode, live, p, parts, size, nq)
        tables = (qt_p, kt_p, kb_p, first_p, mode_p, qstart.astype(jnp.int32))
        state = attend_part(tables, q1, kv_parts[p], qd, qs, kd, ks, state, piece)
    m, l, acc = state
    att1 = (acc / l).astype(jnp.bfloat16)
    att0 = lax.all_to_all(att1, "cg", 0, 0, tiled=True)
    attended = lax.all_to_all(att0, "cl", 0, 1, tiled=True)
    mixed = lax.psum_scatter(
        jnp.dot(attended, out_weight, preferred_element_type=jnp.float32).astype(jnp.bfloat16),
        "tp",
        scatter_dimension=0,
        tiled=True,
    )
    return mixed


def solution(mesh):
    n_ctx = mesh.shape["ctx"]
    n_tp = mesh.shape["tp"]
    group = 4
    inner = Mesh(np.asarray(mesh.devices).reshape(n_ctx // group, group, n_tp), ("cg", "cl", "tp"))
    out_sharding = NamedSharding(mesh, P(("ctx", "tp"), None))
    body = jax.shard_map(
        per_device,
        mesh=inner,
        in_specs=(
            P(("cg", "cl"), "tp"),
            P(("cg", "cl"), "tp"),
            P(("cg", "cl"), "tp"),
            P(),
            P(),
            P(),
            P("tp", None),
        ),
        out_specs=P(("cg", "cl", "tp"), None),
        check_vma=False,
    )

    def run(*args):
        return lax.with_sharding_constraint(body(*args), out_sharding)

    return run
```

```python
import math

import jax
import jax.numpy as jnp
import numpy as np
from jax import lax
from jax.experimental import pallas as pl
from jax.experimental.pallas import tpu as pltpu
from jax.sharding import Mesh, NamedSharding, PartitionSpec as P

HEAD_DIM = 128
BLOCK = 128
DOC_MOST = 80
SPAN_MOST = 4
TK = 512

NEG = -1e30


def block_spans(span_start, span_end, count):
    blocks = jnp.arange(count, dtype=jnp.int32)
    inside = (blocks[:, None] >= span_start[None, :]) & (blocks[:, None] < span_end[None, :])
    labels = jnp.arange(1, span_start.shape[0] + 1, dtype=jnp.int32)
    return jnp.sum(jnp.where(inside, labels[None, :], 0), axis=1) - 1


def make_kernel(tq):
    scale = 1.0 / math.sqrt(HEAD_DIM)

    def kernel(qt_ref, kt_ref, kb_ref, first_ref, mode_ref, qstart_ref,
               q_ref, k_ref, v_ref, qd_ref, qs_ref, kd_ref, ks_ref, m_in, l_in, acc_in,
               m_sc, l_sc, acc_sc):
        p = pl.program_id(0)
        mode = mode_ref[p]

        @pl.when(first_ref[p] == 1)
        def _():
            m_sc[...] = m_in[...]
            l_sc[...] = l_in[...]
            acc_sc[...] = acc_in[...]

        def update(masked):
            scores = lax.dot_general(
                q_ref[...], k_ref[...], (((1,), (1,)), ((), ())), preferred_element_type=jnp.float32
            ) * scale
            m_old = m_sc[...]
            if masked:
                qpos = qstart_ref[qt_ref[p]] + lax.broadcasted_iota(jnp.int32, (tq, TK), 0)
                kpos = kt_ref[p] * TK + lax.broadcasted_iota(jnp.int32, (tq, TK), 1)
                allowed = (qd_ref[...] == kd_ref[...]) & ((kpos <= qpos) | (qs_ref[...] == ks_ref[...]))
                scores = jnp.where(allowed, scores, NEG)
                m_new = jnp.maximum(m_old, jnp.max(scores, axis=1, keepdims=True))
                weights = jnp.where(allowed, jnp.exp(scores - m_new), 0.0)
            else:
                m_new = jnp.maximum(m_old, jnp.max(scores, axis=1, keepdims=True))
                weights = jnp.exp(scores - m_new)
            factor = jnp.exp(m_old - m_new)
            l_sc[...] = l_sc[...] * factor + jnp.sum(weights, axis=1, keepdims=True)
            acc_sc[...] = acc_sc[...] * factor + jnp.dot(
                weights.astype(jnp.bfloat16), v_ref[...], preferred_element_type=jnp.float32
            )
            m_sc[...] = m_new

        @pl.when(mode == 1)
        def _():
            update(True)

        @pl.when(mode == 2)
        def _():
            update(False)

    return kernel


def attend_part(tables, q, kv, qd, qs, kd, ks, state, tq):
    total = tables[0].shape[0]

    def qmap(p, qt, *_):
        return (qt[p], 0)

    def kmap(p, qt, kt, kb, *_):
        return (kb[p], 0)

    def vmap(p, qt, kt, kb, *_):
        return (kb[p], 1)

    def klab(p, qt, kt, *_):
        return (0, kt[p])

    m, l, acc = state
    grid_spec = pltpu.PrefetchScalarGridSpec(
        num_scalar_prefetch=len(tables),
        grid=(total,),
        in_specs=[
            pl.BlockSpec((tq, HEAD_DIM), qmap),
            pl.BlockSpec((TK, HEAD_DIM), kmap),
            pl.BlockSpec((TK, HEAD_DIM), vmap),
            pl.BlockSpec((tq, 1), qmap),
            pl.BlockSpec((tq, 1), qmap),
            pl.BlockSpec((1, TK), klab),
            pl.BlockSpec((1, TK), klab),
            pl.BlockSpec((tq, 1), qmap),
            pl.BlockSpec((tq, 1), qmap),
            pl.BlockSpec((tq, HEAD_DIM), qmap),
        ],
        out_specs=[
            pl.BlockSpec((tq, 1), qmap),
            pl.BlockSpec((tq, 1), qmap),
            pl.BlockSpec((tq, HEAD_DIM), qmap),
        ],
    )
    n = len(tables)
    return pl.pallas_call(
        make_kernel(tq),
        out_shape=(
            jax.ShapeDtypeStruct(m.shape, jnp.float32),
            jax.ShapeDtypeStruct(l.shape, jnp.float32),
            jax.ShapeDtypeStruct(acc.shape, jnp.float32),
        ),
        grid_spec=grid_spec,
        input_output_aliases={n + 7: 0, n + 8: 1, n + 9: 2},
        compiler_params=pltpu.CompilerParams(dimension_semantics=("arbitrary",)),
    )(*tables, q, kv, kv, qd, qs, kd, ks, m, l, acc)


def take(table, index):
    slots = jnp.arange(table.shape[0], dtype=jnp.int32)
    return jnp.sum(jnp.where(index[..., None] == slots, table, 0), axis=-1)


def step_tables(doc_ids, span_blocks, span_end, qstart, tq, seq):
    count = doc_ids.shape[0]
    nq = qstart.shape[0]
    per_q = tq // BLOCK
    per_k = TK // BLOCK
    ntk = seq // TK
    blocks = jnp.arange(count, dtype=jnp.int32)
    same = doc_ids[:, None] == doc_ids[None, :]
    doc_lo = jnp.min(jnp.where(same, blocks[None, :], count), axis=1)
    doc_hi = jnp.max(jnp.where(same, blocks[None, :], -1), axis=1)
    span_hi = jnp.where(span_blocks >= 0, take(span_end, span_blocks) - 1, blocks)
    key_hi = jnp.minimum(jnp.maximum(span_hi, blocks), doc_hi)
    qblocks = (qstart // BLOCK)[:, None] + jnp.arange(per_q, dtype=jnp.int32)[None, :]
    lo_t = jnp.min(take(doc_lo, qblocks), axis=1) // per_k
    hi_t = jnp.max(take(key_hi, qblocks), axis=1) // per_k
    window = (DOC_MOST - 1) + per_q + (SPAN_MOST - 1)
    most = min(ntk, (window - 1) // per_k + 2)
    cnt = jnp.clip(hi_t - lo_t + 1, 1, most)
    ends = jnp.cumsum(cnt)
    starts = ends - cnt
    total = nq * most
    pos = jnp.arange(total, dtype=jnp.int32)
    qt = jnp.minimum(jnp.sum((pos[:, None] >= ends[None, :]).astype(jnp.int32), axis=1), nq - 1)
    live = pos < ends[-1]
    local = jnp.where(live, pos - take(starts, qt), take(cnt, qt) - 1)
    kt = take(lo_t, qt) + local
    first = (live & (local == 0)).astype(jnp.int32)
    last = (live & (local == take(cnt, qt) - 1)).astype(jnp.int32)
    qdoc = take(doc_ids, qblocks)
    kblocks = kt[:, None] * per_k + jnp.arange(per_k, dtype=jnp.int32)[None, :]
    kdoc = take(doc_ids, kblocks)
    qdoc_t = jnp.sum(jnp.where((qt[:, None] == jnp.arange(nq))[:, :, None], qdoc[None], 0), axis=1)
    one_doc = (jnp.min(qdoc_t, axis=1) == jnp.max(qdoc_t, axis=1)) & (
        jnp.min(kdoc, axis=1) == jnp.max(kdoc, axis=1)) & (qdoc_t[:, 0] == kdoc[:, 0])
    below = (kt + 1) * TK - 1 <= take(qstart, qt)
    mode = jnp.where(live, jnp.where(one_doc & below, 2, 1), 0).astype(jnp.int32)
    return qt.astype(jnp.int32), kt.astype(jnp.int32), mode, live, most


def chunk_tables(qt, kt, mode, live, chunk_id, per_chunk, size, nq):
    total = qt.shape[0]
    chosen = live & (kt // per_chunk == chunk_id)
    counts = jnp.cumsum(chosen.astype(jnp.int32))
    n_sel = counts[-1]
    i = jnp.arange(size, dtype=jnp.int32)
    order = jnp.minimum(jnp.sum((counts[None, :] <= i[:, None]).astype(jnp.int32), axis=1), total - 1)
    keep = i < n_sel
    tail = take(order, jnp.maximum(n_sel - 1, 0)[None])[0]
    src = jnp.where(keep, order, tail)
    any_sel = n_sel > 0
    qt_p = jnp.where(any_sel, take(qt, src), nq - 1)
    kt_p = jnp.where(any_sel, take(kt, src), chunk_id * per_chunk)
    mode_p = jnp.where(keep, take(mode, src), 0)
    prev = jnp.concatenate([jnp.full((1,), -1, jnp.int32), qt_p[:-1]])
    first = ((i == 0) | (keep & (qt_p != prev))).astype(jnp.int32)
    return qt_p, kt_p, kt_p - chunk_id * per_chunk, first, mode_p.astype(jnp.int32)


def ring_order(n):
    half = n // 2
    return [2 * y for y in range(half)] + [2 * y + 1 for y in reversed(range(half))]


def per_device(queries, keys, values, doc_ids, span_start, span_end, out_weight):
    rows, local_width = queries.shape
    group = lax.axis_size("cl")
    n_cg = lax.axis_size("cg")
    chunk = rows * group
    piece = chunk // n_cg
    j = lax.axis_index("cg")

    stacked = lax.all_to_all(jnp.stack([queries, keys, values]), "cl", 2, 1, tiled=True)
    q1 = lax.all_to_all(stacked[0], "cg", 0, 0, tiled=True)
    kv1 = jnp.concatenate([stacked[1], stacked[2]], axis=1)
    per_chunk = chunk // TK
    seq = chunk * n_cg
    order = ring_order(n_cg)
    place = [order.index(g) for g in range(n_cg)]
    ring = [(order[i], order[(i + 1) % n_cg]) for i in range(n_cg)]
    order_arr = jnp.asarray(order, jnp.int32)
    my_place = take(jnp.asarray(place, jnp.int32), j[None])[0]

    count = doc_ids.shape[0]
    span_blocks = block_spans(span_start, span_end, count)
    doc_tok = jnp.broadcast_to(doc_ids[:, None], (count, BLOCK)).reshape(seq)
    span_tok = jnp.broadcast_to(span_blocks[:, None], (count, BLOCK)).reshape(seq)
    key_span = jnp.where(span_tok >= 0, span_tok, -2)
    query_span = jnp.where(span_tok >= 0, span_tok, -1)

    def mine(x):
        return lax.dynamic_index_in_dim(x.reshape(n_cg, n_cg, piece), j, axis=1, keepdims=False).reshape(
            chunk, 1)

    qd = mine(doc_tok)
    qs = mine(query_span)
    kd = doc_tok.reshape(1, seq)
    ks = key_span.reshape(1, seq)
    qstart = jnp.arange(n_cg, dtype=jnp.int32) * chunk + j * piece

    qt, kt, mode, live, most = step_tables(doc_ids, span_blocks, span_end, qstart, piece, seq)
    nq = n_cg
    size = nq * per_chunk
    state = (
        jnp.full((chunk, 1), NEG, jnp.float32),
        jnp.zeros((chunk, 1), jnp.float32),
        jnp.zeros((chunk, HEAD_DIM), jnp.float32),
    )
    kv_now = kv1
    for step in range(n_cg):
        if step + 1 < n_cg:
            kv_next = lax.ppermute(kv_now, "cg", ring)
        chunk_id = take(order_arr, ((my_place - step) % n_cg)[None])[0]
        qt_p, kt_p, kb_p, first_p, mode_p = chunk_tables(qt, kt, mode, live, chunk_id, per_chunk, size, nq)
        tables = (qt_p, kt_p, kb_p, first_p, mode_p, qstart.astype(jnp.int32))
        state = attend_part(tables, q1, kv_now, qd, qs, kd, ks, state, piece)
        if step + 1 < n_cg:
            kv_now, state = lax.optimization_barrier((kv_next, state))
    m, l, acc = state
    att1 = (acc / l).astype(jnp.bfloat16)
    att0 = lax.all_to_all(att1, "cg", 0, 0, tiled=True)
    attended = lax.all_to_all(att0, "cl", 0, 1, tiled=True)
    mixed = lax.psum_scatter(
        jnp.dot(attended, out_weight, preferred_element_type=jnp.float32).astype(jnp.bfloat16),
        "tp",
        scatter_dimension=0,
        tiled=True,
    )
    return mixed


def solution(mesh):
    n_ctx = mesh.shape["ctx"]
    n_tp = mesh.shape["tp"]
    group = 4
    inner = Mesh(np.asarray(mesh.devices).reshape(n_ctx // group, group, n_tp), ("cg", "cl", "tp"))
    out_sharding = NamedSharding(mesh, P(("ctx", "tp"), None))
    body = jax.shard_map(
        per_device,
        mesh=inner,
        in_specs=(
            P(("cg", "cl"), "tp"),
            P(("cg", "cl"), "tp"),
            P(("cg", "cl"), "tp"),
            P(),
            P(),
            P(),
            P("tp", None),
        ),
        out_specs=P(("cg", "cl", "tp"), None),
        check_vma=False,
    )

    def run(*args):
        return lax.with_sharding_constraint(body(*args), out_sharding)

    return run
```

```python
import math

import jax
import jax.numpy as jnp
import numpy as np
from jax import lax
from jax.experimental import pallas as pl
from jax.experimental.pallas import tpu as pltpu
from jax.sharding import Mesh, NamedSharding, PartitionSpec as P

HEAD_DIM = 128
BLOCK = 128
DOC_MOST = 80
SPAN_MOST = 4
TK = 512

NEG = -1e30


def block_spans(span_start, span_end, count):
    blocks = jnp.arange(count, dtype=jnp.int32)
    inside = (blocks[:, None] >= span_start[None, :]) & (blocks[:, None] < span_end[None, :])
    labels = jnp.arange(1, span_start.shape[0] + 1, dtype=jnp.int32)
    return jnp.sum(jnp.where(inside, labels[None, :], 0), axis=1) - 1


def make_kernel(tq):
    scale = 1.0 / math.sqrt(HEAD_DIM)

    def kernel(qt_ref, kt_ref, first_ref, last_ref, mode_ref, qstart_ref,
               q_ref, k_ref, v_ref, qd_ref, qs_ref, kd_ref, ks_ref, o_ref, m_sc, l_sc, acc_sc):
        p = pl.program_id(0)
        mode = mode_ref[p]

        @pl.when(first_ref[p] == 1)
        def _():
            m_sc[...] = jnp.full(m_sc.shape, NEG, jnp.float32)
            l_sc[...] = jnp.zeros(l_sc.shape, jnp.float32)
            acc_sc[...] = jnp.zeros(acc_sc.shape, jnp.float32)

        def update(masked):
            scores = lax.dot_general(
                q_ref[...], k_ref[...], (((1,), (1,)), ((), ())), preferred_element_type=jnp.float32
            ) * scale
            m_old = m_sc[...]
            if masked:
                qpos = qstart_ref[qt_ref[p]] + lax.broadcasted_iota(jnp.int32, (tq, TK), 0)
                kpos = kt_ref[p] * TK + lax.broadcasted_iota(jnp.int32, (tq, TK), 1)
                allowed = (qd_ref[...] == kd_ref[...]) & ((kpos <= qpos) | (qs_ref[...] == ks_ref[...]))
                scores = jnp.where(allowed, scores, NEG)
                m_new = jnp.maximum(m_old, jnp.max(scores, axis=1, keepdims=True))
                weights = jnp.where(allowed, jnp.exp(scores - m_new), 0.0)
            else:
                m_new = jnp.maximum(m_old, jnp.max(scores, axis=1, keepdims=True))
                weights = jnp.exp(scores - m_new)
            factor = jnp.exp(m_old - m_new)
            l_sc[...] = l_sc[...] * factor + jnp.sum(weights, axis=1, keepdims=True)
            acc_sc[...] = acc_sc[...] * factor + jnp.dot(
                weights.astype(jnp.bfloat16), v_ref[...], preferred_element_type=jnp.float32
            )
            m_sc[...] = m_new

        @pl.when(mode == 1)
        def _():
            update(True)

        @pl.when(mode == 2)
        def _():
            update(False)

        @pl.when(last_ref[p] == 1)
        def _():
            o_ref[...] = (acc_sc[...] / l_sc[...]).astype(o_ref.dtype)

    return kernel


def attend_head(tables, q, kv, qd, qs, kd, ks, tq):
    total = tables[0].shape[0]

    def qmap(p, qt, kt, *_):
        return (qt[p], 0)

    def kmap(p, qt, kt, *_):
        return (kt[p], 0)

    def vmap(p, qt, kt, *_):
        return (kt[p], 1)

    def klab(p, qt, kt, *_):
        return (0, kt[p])

    grid_spec = pltpu.PrefetchScalarGridSpec(
        num_scalar_prefetch=len(tables),
        grid=(total,),
        in_specs=[
            pl.BlockSpec((tq, HEAD_DIM), qmap),
            pl.BlockSpec((TK, HEAD_DIM), kmap),
            pl.BlockSpec((TK, HEAD_DIM), vmap),
            pl.BlockSpec((tq, 1), qmap),
            pl.BlockSpec((tq, 1), qmap),
            pl.BlockSpec((1, TK), klab),
            pl.BlockSpec((1, TK), klab),
        ],
        out_specs=pl.BlockSpec((tq, HEAD_DIM), qmap),
        scratch_shapes=[
            pltpu.VMEM((tq, 1), jnp.float32),
            pltpu.VMEM((tq, 1), jnp.float32),
            pltpu.VMEM((tq, HEAD_DIM), jnp.float32),
        ],
    )
    return pl.pallas_call(
        make_kernel(tq),
        out_shape=jax.ShapeDtypeStruct(q.shape, jnp.bfloat16),
        grid_spec=grid_spec,
        compiler_params=pltpu.CompilerParams(dimension_semantics=("arbitrary",)),
    )(*tables, q, kv, kv, qd, qs, kd, ks)


def take(table, index):
    slots = jnp.arange(table.shape[0], dtype=jnp.int32)
    return jnp.sum(jnp.where(index[..., None] == slots, table, 0), axis=-1)


def step_tables(doc_ids, span_blocks, span_end, qstart, tq, seq):
    count = doc_ids.shape[0]
    nq = qstart.shape[0]
    per_q = tq // BLOCK
    per_k = TK // BLOCK
    ntk = seq // TK
    blocks = jnp.arange(count, dtype=jnp.int32)
    same = doc_ids[:, None] == doc_ids[None, :]
    doc_lo = jnp.min(jnp.where(same, blocks[None, :], count), axis=1)
    doc_hi = jnp.max(jnp.where(same, blocks[None, :], -1), axis=1)
    span_hi = jnp.where(span_blocks >= 0, take(span_end, span_blocks) - 1, blocks)
    key_hi = jnp.minimum(jnp.maximum(span_hi, blocks), doc_hi)
    qblocks = (qstart // BLOCK)[:, None] + jnp.arange(per_q, dtype=jnp.int32)[None, :]
    lo_t = jnp.min(take(doc_lo, qblocks), axis=1) // per_k
    hi_t = jnp.max(take(key_hi, qblocks), axis=1) // per_k
    window = (DOC_MOST - 1) + per_q + (SPAN_MOST - 1)
    most = min(ntk, (window - 1) // per_k + 2)
    cnt = jnp.clip(hi_t - lo_t + 1, 1, most)
    ends = jnp.cumsum(cnt)
    starts = ends - cnt
    total = nq * most
    pos = jnp.arange(total, dtype=jnp.int32)
    qt = jnp.minimum(jnp.sum((pos[:, None] >= ends[None, :]).astype(jnp.int32), axis=1), nq - 1)
    live = pos < ends[-1]
    local = jnp.where(live, pos - take(starts, qt), take(cnt, qt) - 1)
    kt = take(lo_t, qt) + local
    first = (live & (local == 0)).astype(jnp.int32)
    last = (live & (local == take(cnt, qt) - 1)).astype(jnp.int32)
    qdoc = take(doc_ids, qblocks)
    kblocks = kt[:, None] * per_k + jnp.arange(per_k, dtype=jnp.int32)[None, :]
    kdoc = take(doc_ids, kblocks)
    qdoc_t = jnp.sum(jnp.where((qt[:, None] == jnp.arange(nq))[:, :, None], qdoc[None], 0), axis=1)
    one_doc = (jnp.min(qdoc_t, axis=1) == jnp.max(qdoc_t, axis=1)) & (
        jnp.min(kdoc, axis=1) == jnp.max(kdoc, axis=1)) & (qdoc_t[:, 0] == kdoc[:, 0])
    below = (kt + 1) * TK - 1 <= take(qstart, qt)
    mode = jnp.where(live, jnp.where(one_doc & below, 2, 1), 0).astype(jnp.int32)
    return (qt.astype(jnp.int32), kt.astype(jnp.int32), first, last, mode, qstart.astype(jnp.int32))


def per_device(queries, keys, values, doc_ids, span_start, span_end, out_weight):
    rows, local_width = queries.shape
    group = lax.axis_size("cl")
    n_cg = lax.axis_size("cg")
    chunk = rows * group
    piece = chunk // n_cg
    j = lax.axis_index("cg")

    stacked = lax.all_to_all(jnp.stack([queries, keys, values]), "cl", 2, 1, tiled=True)
    q1 = lax.all_to_all(stacked[0], "cg", 0, 0, tiled=True)
    kv1 = jnp.concatenate([stacked[1], stacked[2]], axis=1)
    kv_all = lax.all_gather(kv1, "cg", axis=0, tiled=True)
    seq = kv_all.shape[0]

    count = doc_ids.shape[0]
    span_blocks = block_spans(span_start, span_end, count)
    doc_tok = jnp.broadcast_to(doc_ids[:, None], (count, BLOCK)).reshape(seq)
    span_tok = jnp.broadcast_to(span_blocks[:, None], (count, BLOCK)).reshape(seq)
    key_span = jnp.where(span_tok >= 0, span_tok, -2)
    query_span = jnp.where(span_tok >= 0, span_tok, -1)

    def mine(x):
        return lax.dynamic_index_in_dim(x.reshape(n_cg, n_cg, piece), j, axis=1, keepdims=False).reshape(
            chunk, 1)

    qd = mine(doc_tok)
    qs = mine(query_span)
    kd = doc_tok.reshape(1, seq)
    ks = key_span.reshape(1, seq)
    qstart = jnp.arange(n_cg, dtype=jnp.int32) * chunk + j * piece

    tables = step_tables(doc_ids, span_blocks, span_end, qstart, piece, seq)
    att1 = attend_head(tables, q1, kv_all, qd, qs, kd, ks, piece)
    att0 = lax.all_to_all(att1, "cg", 0, 0, tiled=True)
    attended = lax.all_to_all(att0, "cl", 0, 1, tiled=True)
    tc = lax.axis_index("tc")
    th = lax.axis_index("th")
    swap = [(0, 1), (1, 0)]
    w_other = lax.ppermute(out_weight, "tc", swap)
    w_pair = jnp.where(tc == 0, jnp.concatenate([out_weight, w_other], axis=0),
                       jnp.concatenate([w_other, out_weight], axis=0))
    quarter = rows // 4
    blocks = attended.reshape(2, 2, quarter, local_width)
    keep = lax.dynamic_index_in_dim(blocks, tc, axis=1, keepdims=False)
    give = lax.dynamic_index_in_dim(blocks, 1 - tc, axis=1, keepdims=False)
    got = lax.ppermute(give, "tc", swap)
    a_pair = jnp.where(tc == 0, jnp.concatenate([keep, got], axis=2), jnp.concatenate([got, keep], axis=2))
    partial = jnp.dot(a_pair.reshape(2 * quarter, 2 * local_width), w_pair,
                      preferred_element_type=jnp.float32).reshape(2, quarter, -1)
    mine_half = lax.dynamic_index_in_dim(partial, th, axis=0, keepdims=False)
    other_half = lax.dynamic_index_in_dim(partial, 1 - th, axis=0, keepdims=False).astype(jnp.bfloat16)
    recv = lax.ppermute(other_half, "th", swap)
    return (mine_half + recv.astype(jnp.float32)).astype(jnp.bfloat16)


def solution(mesh):
    n_ctx = mesh.shape["ctx"]
    group = 4
    inner = Mesh(np.asarray(mesh.devices).reshape(n_ctx // group, group, 2, 2), ("cg", "cl", "th", "tc"))
    out_sharding = NamedSharding(mesh, P(("ctx", "tp"), None))
    split = P(("cg", "cl"), ("th", "tc"))
    body = jax.shard_map(
        per_device,
        mesh=inner,
        in_specs=(split, split, split, P(), P(), P(), P(("th", "tc"), None)),
        out_specs=P(("cg", "cl", "th", "tc"), None),
        check_vma=False,
    )

    def run(*args):
        return lax.with_sharding_constraint(body(*args), out_sharding)

    return run
```

```python
import math

import jax
import jax.numpy as jnp
import numpy as np
from jax import lax
from jax.experimental import pallas as pl
from jax.experimental.pallas import tpu as pltpu
from jax.sharding import Mesh, NamedSharding, PartitionSpec as P

HEAD_DIM = 128
BLOCK = 128
DOC_MOST = 80
SPAN_MOST = 4
TK = 512

NEG = -1e30


def block_spans(span_start, span_end, count):
    blocks = jnp.arange(count, dtype=jnp.int32)
    inside = (blocks[:, None] >= span_start[None, :]) & (blocks[:, None] < span_end[None, :])
    labels = jnp.arange(1, span_start.shape[0] + 1, dtype=jnp.int32)
    return jnp.sum(jnp.where(inside, labels[None, :], 0), axis=1) - 1


def make_kernel(tq):
    scale = 1.0 / math.sqrt(HEAD_DIM)

    def kernel(qt_ref, kt_ref, first_ref, last_ref, mode_ref, qstart_ref,
               q_ref, k_ref, v_ref, qd_ref, qs_ref, kd_ref, ks_ref, o_ref, m_sc, l_sc, acc_sc):
        p = pl.program_id(0)
        mode = mode_ref[p]

        @pl.when(first_ref[p] == 1)
        def _():
            m_sc[...] = jnp.full(m_sc.shape, NEG, jnp.float32)
            l_sc[...] = jnp.zeros(l_sc.shape, jnp.float32)
            acc_sc[...] = jnp.zeros(acc_sc.shape, jnp.float32)

        def update(masked):
            scores = lax.dot_general(
                q_ref[...], k_ref[...], (((1,), (1,)), ((), ())), preferred_element_type=jnp.float32
            ) * scale
            m_old = m_sc[...]
            if masked:
                qpos = qstart_ref[qt_ref[p]] + lax.broadcasted_iota(jnp.int32, (tq, TK), 0)
                kpos = kt_ref[p] * TK + lax.broadcasted_iota(jnp.int32, (tq, TK), 1)
                allowed = (qd_ref[...] == kd_ref[...]) & ((kpos <= qpos) | (qs_ref[...] == ks_ref[...]))
                scores = jnp.where(allowed, scores, NEG)
                m_new = jnp.maximum(m_old, jnp.max(scores, axis=1, keepdims=True))
                weights = jnp.where(allowed, jnp.exp(scores - m_new), 0.0)
            else:
                m_new = jnp.maximum(m_old, jnp.max(scores, axis=1, keepdims=True))
                weights = jnp.exp(scores - m_new)
            factor = jnp.exp(m_old - m_new)
            l_sc[...] = l_sc[...] * factor + jnp.sum(weights, axis=1, keepdims=True)
            acc_sc[...] = acc_sc[...] * factor + jnp.dot(
                weights.astype(jnp.bfloat16), v_ref[...], preferred_element_type=jnp.float32
            )
            m_sc[...] = m_new

        @pl.when(mode == 1)
        def _():
            update(True)

        @pl.when(mode == 2)
        def _():
            update(False)

        @pl.when(last_ref[p] == 1)
        def _():
            o_ref[...] = (acc_sc[...] / l_sc[...]).astype(o_ref.dtype)

    return kernel


def attend_head(tables, q, k, v, qd, qs, kd, ks, tq):
    total = tables[0].shape[0]

    def qmap(p, qt, kt, *_):
        return (qt[p], 0)

    def kmap(p, qt, kt, *_):
        return (kt[p], 0)

    def vmap(p, qt, kt, *_):
        return (kt[p], 0)

    def klab(p, qt, kt, *_):
        return (0, kt[p])

    grid_spec = pltpu.PrefetchScalarGridSpec(
        num_scalar_prefetch=len(tables),
        grid=(total,),
        in_specs=[
            pl.BlockSpec((tq, HEAD_DIM), qmap),
            pl.BlockSpec((TK, HEAD_DIM), kmap),
            pl.BlockSpec((TK, HEAD_DIM), vmap),
            pl.BlockSpec((tq, 1), qmap),
            pl.BlockSpec((tq, 1), qmap),
            pl.BlockSpec((1, TK), klab),
            pl.BlockSpec((1, TK), klab),
        ],
        out_specs=pl.BlockSpec((tq, HEAD_DIM), qmap),
        scratch_shapes=[
            pltpu.VMEM((tq, 1), jnp.float32),
            pltpu.VMEM((tq, 1), jnp.float32),
            pltpu.VMEM((tq, HEAD_DIM), jnp.float32),
        ],
    )
    return pl.pallas_call(
        make_kernel(tq),
        out_shape=jax.ShapeDtypeStruct(q.shape, jnp.bfloat16),
        grid_spec=grid_spec,
        compiler_params=pltpu.CompilerParams(dimension_semantics=("arbitrary",)),
    )(*tables, q, k, v, qd, qs, kd, ks)


def take(table, index):
    slots = jnp.arange(table.shape[0], dtype=jnp.int32)
    return jnp.sum(jnp.where(index[..., None] == slots, table, 0), axis=-1)


def step_tables(doc_ids, span_blocks, span_end, qstart, tq, seq):
    count = doc_ids.shape[0]
    nq = qstart.shape[0]
    per_q = tq // BLOCK
    per_k = TK // BLOCK
    ntk = seq // TK
    blocks = jnp.arange(count, dtype=jnp.int32)
    same = doc_ids[:, None] == doc_ids[None, :]
    doc_lo = jnp.min(jnp.where(same, blocks[None, :], count), axis=1)
    doc_hi = jnp.max(jnp.where(same, blocks[None, :], -1), axis=1)
    span_hi = jnp.where(span_blocks >= 0, take(span_end, span_blocks) - 1, blocks)
    key_hi = jnp.minimum(jnp.maximum(span_hi, blocks), doc_hi)
    qblocks = (qstart // BLOCK)[:, None] + jnp.arange(per_q, dtype=jnp.int32)[None, :]
    lo_t = jnp.min(take(doc_lo, qblocks), axis=1) // per_k
    hi_t = jnp.max(take(key_hi, qblocks), axis=1) // per_k
    window = (DOC_MOST - 1) + per_q + (SPAN_MOST - 1)
    most = min(ntk, (window - 1) // per_k + 2)
    cnt = jnp.clip(hi_t - lo_t + 1, 1, most)
    ends = jnp.cumsum(cnt)
    starts = ends - cnt
    total = nq * most
    pos = jnp.arange(total, dtype=jnp.int32)
    qt = jnp.minimum(jnp.sum((pos[:, None] >= ends[None, :]).astype(jnp.int32), axis=1), nq - 1)
    live = pos < ends[-1]
    local = jnp.where(live, pos - take(starts, qt), take(cnt, qt) - 1)
    kt = take(lo_t, qt) + local
    first = (live & (local == 0)).astype(jnp.int32)
    last = (live & (local == take(cnt, qt) - 1)).astype(jnp.int32)
    qdoc = take(doc_ids, qblocks)
    kblocks = kt[:, None] * per_k + jnp.arange(per_k, dtype=jnp.int32)[None, :]
    kdoc = take(doc_ids, kblocks)
    qdoc_t = jnp.sum(jnp.where((qt[:, None] == jnp.arange(nq))[:, :, None], qdoc[None], 0), axis=1)
    one_doc = (jnp.min(qdoc_t, axis=1) == jnp.max(qdoc_t, axis=1)) & (
        jnp.min(kdoc, axis=1) == jnp.max(kdoc, axis=1)) & (qdoc_t[:, 0] == kdoc[:, 0])
    below = (kt + 1) * TK - 1 <= take(qstart, qt)
    mode = jnp.where(live, jnp.where(one_doc & below, 2, 1), 0).astype(jnp.int32)
    return (qt.astype(jnp.int32), kt.astype(jnp.int32), first, last, mode, qstart.astype(jnp.int32))


def shifted(x, axis, s):
    n = lax.axis_size(axis)
    return lax.ppermute(x, axis, [(i, (i + s) % n) for i in range(n)])


def gathered(x, axis):
    n = lax.axis_size(axis)
    me = lax.axis_index(axis)
    size = x.shape[0]
    out = jnp.zeros((size * n,) + x.shape[1:], x.dtype)
    for s in range(n):
        got = x if s == 0 else shifted(x, axis, s)
        out = lax.dynamic_update_slice_in_dim(out, got, ((me - s) % n) * size, 0)
    return out


def per_device(queries, keys, values, doc_ids, span_start, span_end, out_weight):
    rows, local_width = queries.shape
    group = lax.axis_size("cl")
    n_cg = lax.axis_size("cg")
    chunk = rows * group
    piece = chunk // n_cg
    j = lax.axis_index("cg")

    stacked = lax.all_to_all(jnp.stack([queries, keys, values]), "cl", 2, 1, tiled=True)
    q1 = lax.all_to_all(stacked[0], "cg", 0, 0, tiled=True)
    k_all = lax.all_gather(stacked[1], "cg", axis=0, tiled=True)
    v_all = gathered(stacked[2], "cg")
    seq = k_all.shape[0]

    count = doc_ids.shape[0]
    span_blocks = block_spans(span_start, span_end, count)
    doc_tok = jnp.broadcast_to(doc_ids[:, None], (count, BLOCK)).reshape(seq)
    span_tok = jnp.broadcast_to(span_blocks[:, None], (count, BLOCK)).reshape(seq)
    key_span = jnp.where(span_tok >= 0, span_tok, -2)
    query_span = jnp.where(span_tok >= 0, span_tok, -1)

    def mine(x):
        return lax.dynamic_index_in_dim(x.reshape(n_cg, n_cg, piece), j, axis=1, keepdims=False).reshape(
            chunk, 1)

    qd = mine(doc_tok)
    qs = mine(query_span)
    kd = doc_tok.reshape(1, seq)
    ks = key_span.reshape(1, seq)
    qstart = jnp.arange(n_cg, dtype=jnp.int32) * chunk + j * piece

    tables = step_tables(doc_ids, span_blocks, span_end, qstart, piece, seq)
    att1 = attend_head(tables, q1, k_all, v_all, qd, qs, kd, ks, piece)
    att0 = lax.all_to_all(att1, "cg", 0, 0, tiled=True)
    attended = lax.all_to_all(att0, "cl", 0, 1, tiled=True)
    tc = lax.axis_index("tc")
    th = lax.axis_index("th")
    swap = [(0, 1), (1, 0)]
    w_other = lax.ppermute(out_weight, "tc", swap)
    w_pair = jnp.where(tc == 0, jnp.concatenate([out_weight, w_other], axis=0),
                       jnp.concatenate([w_other, out_weight], axis=0))
    quarter = rows // 4
    blocks = attended.reshape(2, 2, quarter, local_width)
    keep = lax.dynamic_index_in_dim(blocks, tc, axis=1, keepdims=False)
    give = lax.dynamic_index_in_dim(blocks, 1 - tc, axis=1, keepdims=False)
    got = lax.ppermute(give, "tc", swap)
    a_pair = jnp.where(tc == 0, jnp.concatenate([keep, got], axis=2), jnp.concatenate([got, keep], axis=2))
    partial = jnp.dot(a_pair.reshape(2 * quarter, 2 * local_width), w_pair,
                      preferred_element_type=jnp.float32).reshape(2, quarter, -1)
    mine_half = lax.dynamic_index_in_dim(partial, th, axis=0, keepdims=False)
    other_half = lax.dynamic_index_in_dim(partial, 1 - th, axis=0, keepdims=False).astype(jnp.bfloat16)
    recv = lax.ppermute(other_half, "th", swap)
    return (mine_half + recv.astype(jnp.float32)).astype(jnp.bfloat16)


def solution(mesh):
    n_ctx = mesh.shape["ctx"]
    group = 4
    inner = Mesh(np.asarray(mesh.devices).reshape(n_ctx // group, group, 2, 2), ("cg", "cl", "th", "tc"))
    out_sharding = NamedSharding(mesh, P(("ctx", "tp"), None))
    split = P(("cg", "cl"), ("th", "tc"))
    body = jax.shard_map(
        per_device,
        mesh=inner,
        in_specs=(split, split, split, P(), P(), P(), P(("th", "tc"), None)),
        out_specs=P(("cg", "cl", "th", "tc"), None),
        check_vma=False,
    )

    def run(*args):
        return lax.with_sharding_constraint(body(*args), out_sharding)

    return run
```

```python
import math

import jax
import jax.numpy as jnp
import numpy as np
from jax import lax
from jax.experimental import pallas as pl
from jax.experimental.pallas import tpu as pltpu
from jax.sharding import Mesh, NamedSharding, PartitionSpec as P

HEAD_DIM = 128
BLOCK = 128
DOC_MOST = 80
SPAN_MOST = 4
TK = 512

NEG = -1e30


def block_spans(span_start, span_end, count):
    blocks = jnp.arange(count, dtype=jnp.int32)
    inside = (blocks[:, None] >= span_start[None, :]) & (blocks[:, None] < span_end[None, :])
    labels = jnp.arange(1, span_start.shape[0] + 1, dtype=jnp.int32)
    return jnp.sum(jnp.where(inside, labels[None, :], 0), axis=1) - 1


def make_kernel(tq):
    scale = 1.0 / math.sqrt(HEAD_DIM)

    def kernel(qt_ref, kt_ref, first_ref, last_ref, mode_ref, qstart_ref,
               q_ref, k_ref, v_ref, qd_ref, qs_ref, kd_ref, ks_ref, o_ref, m_sc, l_sc, acc_sc):
        p = pl.program_id(0)
        mode = mode_ref[p]

        @pl.when(first_ref[p] == 1)
        def _():
            m_sc[...] = jnp.full(m_sc.shape, NEG, jnp.float32)
            l_sc[...] = jnp.zeros(l_sc.shape, jnp.float32)
            acc_sc[...] = jnp.zeros(acc_sc.shape, jnp.float32)

        def update(masked):
            scores = lax.dot_general(
                q_ref[...], k_ref[...], (((1,), (1,)), ((), ())), preferred_element_type=jnp.float32
            ) * scale
            m_old = m_sc[...]
            if masked:
                qpos = qstart_ref[qt_ref[p]] + lax.broadcasted_iota(jnp.int32, (tq, TK), 0)
                kpos = kt_ref[p] * TK + lax.broadcasted_iota(jnp.int32, (tq, TK), 1)
                allowed = (qd_ref[...] == kd_ref[...]) & ((kpos <= qpos) | (qs_ref[...] == ks_ref[...]))
                scores = jnp.where(allowed, scores, NEG)
                m_new = jnp.maximum(m_old, jnp.max(scores, axis=1, keepdims=True))
                weights = jnp.where(allowed, jnp.exp(scores - m_new), 0.0)
            else:
                m_new = jnp.maximum(m_old, jnp.max(scores, axis=1, keepdims=True))
                weights = jnp.exp(scores - m_new)
            factor = jnp.exp(m_old - m_new)
            l_sc[...] = l_sc[...] * factor + jnp.sum(weights, axis=1, keepdims=True)
            acc_sc[...] = acc_sc[...] * factor + jnp.dot(
                weights.astype(jnp.bfloat16), v_ref[...], preferred_element_type=jnp.float32
            )
            m_sc[...] = m_new

        @pl.when(mode == 1)
        def _():
            update(True)

        @pl.when(mode == 2)
        def _():
            update(False)

        @pl.when(last_ref[p] == 1)
        def _():
            o_ref[...] = (acc_sc[...] / l_sc[...]).astype(o_ref.dtype)

    return kernel


def attend_head(tables, q, kv, qd, qs, kd, ks, tq):
    total = tables[0].shape[0]

    def qmap(p, qt, kt, *_):
        return (qt[p], 0)

    def kmap(p, qt, kt, *_):
        return (kt[p], 0)

    def vmap(p, qt, kt, *_):
        return (kt[p], 1)

    def klab(p, qt, kt, *_):
        return (0, kt[p])

    grid_spec = pltpu.PrefetchScalarGridSpec(
        num_scalar_prefetch=len(tables),
        grid=(total,),
        in_specs=[
            pl.BlockSpec((tq, HEAD_DIM), qmap),
            pl.BlockSpec((TK, HEAD_DIM), kmap),
            pl.BlockSpec((TK, HEAD_DIM), vmap),
            pl.BlockSpec((tq, 1), qmap),
            pl.BlockSpec((tq, 1), qmap),
            pl.BlockSpec((1, TK), klab),
            pl.BlockSpec((1, TK), klab),
        ],
        out_specs=pl.BlockSpec((tq, HEAD_DIM), qmap),
        scratch_shapes=[
            pltpu.VMEM((tq, 1), jnp.float32),
            pltpu.VMEM((tq, 1), jnp.float32),
            pltpu.VMEM((tq, HEAD_DIM), jnp.float32),
        ],
    )
    return pl.pallas_call(
        make_kernel(tq),
        out_shape=jax.ShapeDtypeStruct(q.shape, jnp.bfloat16),
        grid_spec=grid_spec,
        compiler_params=pltpu.CompilerParams(dimension_semantics=("arbitrary",)),
    )(*tables, q, kv, kv, qd, qs, kd, ks)


def take(table, index):
    slots = jnp.arange(table.shape[0], dtype=jnp.int32)
    return jnp.sum(jnp.where(index[..., None] == slots, table, 0), axis=-1)


def step_tables(doc_ids, span_blocks, span_end, qstart, tq, seq):
    count = doc_ids.shape[0]
    nq = qstart.shape[0]
    per_q = tq // BLOCK
    per_k = TK // BLOCK
    ntk = seq // TK
    blocks = jnp.arange(count, dtype=jnp.int32)
    same = doc_ids[:, None] == doc_ids[None, :]
    doc_lo = jnp.min(jnp.where(same, blocks[None, :], count), axis=1)
    doc_hi = jnp.max(jnp.where(same, blocks[None, :], -1), axis=1)
    span_hi = jnp.where(span_blocks >= 0, take(span_end, span_blocks) - 1, blocks)
    key_hi = jnp.minimum(jnp.maximum(span_hi, blocks), doc_hi)
    qblocks = (qstart // BLOCK)[:, None] + jnp.arange(per_q, dtype=jnp.int32)[None, :]
    lo_t = jnp.min(take(doc_lo, qblocks), axis=1) // per_k
    hi_t = jnp.max(take(key_hi, qblocks), axis=1) // per_k
    window = (DOC_MOST - 1) + per_q + (SPAN_MOST - 1)
    most = min(ntk, (window - 1) // per_k + 2)
    cnt = jnp.clip(hi_t - lo_t + 1, 1, most)
    ends = jnp.cumsum(cnt)
    starts = ends - cnt
    total = nq * most
    pos = jnp.arange(total, dtype=jnp.int32)
    qt = jnp.minimum(jnp.sum((pos[:, None] >= ends[None, :]).astype(jnp.int32), axis=1), nq - 1)
    live = pos < ends[-1]
    local = jnp.where(live, pos - take(starts, qt), take(cnt, qt) - 1)
    kt = take(lo_t, qt) + local
    first = (live & (local == 0)).astype(jnp.int32)
    last = (live & (local == take(cnt, qt) - 1)).astype(jnp.int32)
    qdoc = take(doc_ids, qblocks)
    kblocks = kt[:, None] * per_k + jnp.arange(per_k, dtype=jnp.int32)[None, :]
    kdoc = take(doc_ids, kblocks)
    qdoc_t = jnp.sum(jnp.where((qt[:, None] == jnp.arange(nq))[:, :, None], qdoc[None], 0), axis=1)
    one_doc = (jnp.min(qdoc_t, axis=1) == jnp.max(qdoc_t, axis=1)) & (
        jnp.min(kdoc, axis=1) == jnp.max(kdoc, axis=1)) & (qdoc_t[:, 0] == kdoc[:, 0])
    below = (kt + 1) * TK - 1 <= take(qstart, qt)
    mode = jnp.where(live, jnp.where(one_doc & below, 2, 1), 0).astype(jnp.int32)
    return (qt.astype(jnp.int32), kt.astype(jnp.int32), first, last, mode, qstart.astype(jnp.int32))


def per_device(queries, keys, values, doc_ids, span_start, span_end, out_weight):
    rows, local_width = queries.shape
    group = lax.axis_size("cl")
    n_cg = lax.axis_size("cg")
    chunk = rows * group
    piece = chunk // n_cg
    j = lax.axis_index("cg")

    stacked = lax.all_to_all(jnp.stack([keys, values]), "cl", 2, 1, tiled=True)
    kv1 = jnp.concatenate([stacked[0], stacked[1]], axis=1)
    kv_all = lax.all_gather(kv1, "cg", axis=0, tiled=True)
    q1 = lax.all_to_all(lax.all_to_all(queries, "cl", 1, 0, tiled=True), "cg", 0, 0, tiled=True)
    seq = kv_all.shape[0]

    count = doc_ids.shape[0]
    span_blocks = block_spans(span_start, span_end, count)
    doc_tok = jnp.broadcast_to(doc_ids[:, None], (count, BLOCK)).reshape(seq)
    span_tok = jnp.broadcast_to(span_blocks[:, None], (count, BLOCK)).reshape(seq)
    key_span = jnp.where(span_tok >= 0, span_tok, -2)
    query_span = jnp.where(span_tok >= 0, span_tok, -1)

    def mine(x):
        return lax.dynamic_index_in_dim(x.reshape(n_cg, n_cg, piece), j, axis=1, keepdims=False).reshape(
            chunk, 1)

    qd = mine(doc_tok)
    qs = mine(query_span)
    kd = doc_tok.reshape(1, seq)
    ks = key_span.reshape(1, seq)
    qstart = jnp.arange(n_cg, dtype=jnp.int32) * chunk + j * piece

    tables = step_tables(doc_ids, span_blocks, span_end, qstart, piece, seq)
    att1 = attend_head(tables, q1, kv_all, qd, qs, kd, ks, piece)
    att0 = lax.all_to_all(att1, "cg", 0, 0, tiled=True)
    attended = lax.all_to_all(att0, "cl", 0, 1, tiled=True)
    tc = lax.axis_index("tc")
    th = lax.axis_index("th")
    swap = [(0, 1), (1, 0)]
    w_other = lax.ppermute(out_weight, "tc", swap)
    w_pair = jnp.where(tc == 0, jnp.concatenate([out_weight, w_other], axis=0),
                       jnp.concatenate([w_other, out_weight], axis=0))
    quarter = rows // 4
    blocks = attended.reshape(2, 2, quarter, local_width)
    keep = lax.dynamic_index_in_dim(blocks, tc, axis=1, keepdims=False)
    give = lax.dynamic_index_in_dim(blocks, 1 - tc, axis=1, keepdims=False)
    got = lax.ppermute(give, "tc", swap)
    a_pair = jnp.where(tc == 0, jnp.concatenate([keep, got], axis=2), jnp.concatenate([got, keep], axis=2))
    partial = jnp.dot(a_pair.reshape(2 * quarter, 2 * local_width), w_pair,
                      preferred_element_type=jnp.float32).reshape(2, quarter, -1)
    mine_half = lax.dynamic_index_in_dim(partial, th, axis=0, keepdims=False)
    other_half = lax.dynamic_index_in_dim(partial, 1 - th, axis=0, keepdims=False).astype(jnp.bfloat16)
    recv = lax.ppermute(other_half, "th", swap)
    return (mine_half + recv.astype(jnp.float32)).astype(jnp.bfloat16)


def solution(mesh):
    n_ctx = mesh.shape["ctx"]
    group = 4
    inner = Mesh(np.asarray(mesh.devices).reshape(n_ctx // group, group, 2, 2), ("cg", "cl", "th", "tc"))
    out_sharding = NamedSharding(mesh, P(("ctx", "tp"), None))
    split = P(("cg", "cl"), ("th", "tc"))
    body = jax.shard_map(
        per_device,
        mesh=inner,
        in_specs=(split, split, split, P(), P(), P(), P(("th", "tc"), None)),
        out_specs=P(("cg", "cl", "th", "tc"), None),
        check_vma=False,
    )

    def run(*args):
        return lax.with_sharding_constraint(body(*args), out_sharding)

    return run
```

```python
import math

import jax
import jax.numpy as jnp
import numpy as np
from jax import lax
from jax.experimental import pallas as pl
from jax.experimental.pallas import tpu as pltpu
from jax.sharding import Mesh, NamedSharding, PartitionSpec as P

HEAD_DIM = 128
BLOCK = 128
DOC_MOST = 80
SPAN_MOST = 4
TK = 512

NEG = -1e30


def block_spans(span_start, span_end, count):
    blocks = jnp.arange(count, dtype=jnp.int32)
    inside = (blocks[:, None] >= span_start[None, :]) & (blocks[:, None] < span_end[None, :])
    labels = jnp.arange(1, span_start.shape[0] + 1, dtype=jnp.int32)
    return jnp.sum(jnp.where(inside, labels[None, :], 0), axis=1) - 1


def make_kernel(tq):
    scale = 1.0 / math.sqrt(HEAD_DIM)

    def kernel(qt_ref, kt_ref, first_ref, last_ref, mode_ref, qstart_ref,
               q_ref, k_ref, v_ref, qd_ref, qs_ref, kd_ref, ks_ref, o_ref, m_sc, l_sc, acc_sc):
        p = pl.program_id(0)
        mode = mode_ref[p]

        @pl.when(first_ref[p] == 1)
        def _():
            m_sc[...] = jnp.full(m_sc.shape, NEG, jnp.float32)
            l_sc[...] = jnp.zeros(l_sc.shape, jnp.float32)
            acc_sc[...] = jnp.zeros(acc_sc.shape, jnp.float32)

        def update(masked):
            scores = lax.dot_general(
                q_ref[...], k_ref[...], (((1,), (1,)), ((), ())), preferred_element_type=jnp.float32
            ) * scale
            m_old = m_sc[...]
            if masked:
                qpos = qstart_ref[qt_ref[p]] + lax.broadcasted_iota(jnp.int32, (tq, TK), 0)
                kpos = kt_ref[p] * TK + lax.broadcasted_iota(jnp.int32, (tq, TK), 1)
                allowed = (qd_ref[...] == kd_ref[...]) & ((kpos <= qpos) | (qs_ref[...] == ks_ref[...]))
                scores = jnp.where(allowed, scores, NEG)
                m_new = jnp.maximum(m_old, jnp.max(scores, axis=1, keepdims=True))
                weights = jnp.where(allowed, jnp.exp(scores - m_new), 0.0)
            else:
                m_new = jnp.maximum(m_old, jnp.max(scores, axis=1, keepdims=True))
                weights = jnp.exp(scores - m_new)
            factor = jnp.exp(m_old - m_new)
            l_sc[...] = l_sc[...] * factor + jnp.sum(weights, axis=1, keepdims=True)
            acc_sc[...] = acc_sc[...] * factor + jnp.dot(
                weights.astype(jnp.bfloat16), v_ref[...], preferred_element_type=jnp.float32
            )
            m_sc[...] = m_new

        @pl.when(mode == 1)
        def _():
            update(True)

        @pl.when(mode == 2)
        def _():
            update(False)

        @pl.when(last_ref[p] == 1)
        def _():
            o_ref[...] = (acc_sc[...] / l_sc[...]).astype(o_ref.dtype)

    return kernel


def attend_head(tables, q, kv, qd, qs, kd, ks, tq):
    total = tables[0].shape[0]

    def qmap(p, qt, kt, *_):
        return (qt[p], 0)

    def kmap(p, qt, kt, *_):
        return (kt[p], 0)

    def vmap(p, qt, kt, *_):
        return (kt[p], 1)

    def klab(p, qt, kt, *_):
        return (0, kt[p])

    grid_spec = pltpu.PrefetchScalarGridSpec(
        num_scalar_prefetch=len(tables),
        grid=(total,),
        in_specs=[
            pl.BlockSpec((tq, HEAD_DIM), qmap),
            pl.BlockSpec((TK, HEAD_DIM), kmap),
            pl.BlockSpec((TK, HEAD_DIM), vmap),
            pl.BlockSpec((tq, 1), qmap),
            pl.BlockSpec((tq, 1), qmap),
            pl.BlockSpec((1, TK), klab),
            pl.BlockSpec((1, TK), klab),
        ],
        out_specs=pl.BlockSpec((tq, HEAD_DIM), qmap),
        scratch_shapes=[
            pltpu.VMEM((tq, 1), jnp.float32),
            pltpu.VMEM((tq, 1), jnp.float32),
            pltpu.VMEM((tq, HEAD_DIM), jnp.float32),
        ],
    )
    return pl.pallas_call(
        make_kernel(tq),
        out_shape=jax.ShapeDtypeStruct(q.shape, jnp.bfloat16),
        grid_spec=grid_spec,
        compiler_params=pltpu.CompilerParams(dimension_semantics=("arbitrary",)),
    )(*tables, q, kv, kv, qd, qs, kd, ks)


def take(table, index):
    slots = jnp.arange(table.shape[0], dtype=jnp.int32)
    return jnp.sum(jnp.where(index[..., None] == slots, table, 0), axis=-1)


def step_tables(doc_ids, span_blocks, span_end, qstart, tq, seq):
    count = doc_ids.shape[0]
    nq = qstart.shape[0]
    per_q = tq // BLOCK
    per_k = TK // BLOCK
    ntk = seq // TK
    blocks = jnp.arange(count, dtype=jnp.int32)
    same = doc_ids[:, None] == doc_ids[None, :]
    doc_lo = jnp.min(jnp.where(same, blocks[None, :], count), axis=1)
    doc_hi = jnp.max(jnp.where(same, blocks[None, :], -1), axis=1)
    span_hi = jnp.where(span_blocks >= 0, take(span_end, span_blocks) - 1, blocks)
    key_hi = jnp.minimum(jnp.maximum(span_hi, blocks), doc_hi)
    qblocks = (qstart // BLOCK)[:, None] + jnp.arange(per_q, dtype=jnp.int32)[None, :]
    lo_t = jnp.min(take(doc_lo, qblocks), axis=1) // per_k
    hi_t = jnp.max(take(key_hi, qblocks), axis=1) // per_k
    window = (DOC_MOST - 1) + per_q + (SPAN_MOST - 1)
    most = min(ntk, (window - 1) // per_k + 2)
    cnt = jnp.clip(hi_t - lo_t + 1, 1, most)
    ends = jnp.cumsum(cnt)
    starts = ends - cnt
    stride = seq // nq // BLOCK
    rest, spread = count, 0
    while rest > 0:
        size = min(DOC_MOST, rest)
        spread += sum(max(0, size - 1 - stride * i) for i in range(size // stride + 1))
        rest -= size
    total = min(nq * most, nq * 3 + spread // per_k + 1)
    pos = jnp.arange(total, dtype=jnp.int32)
    qt = jnp.minimum(jnp.sum((pos[:, None] >= ends[None, :]).astype(jnp.int32), axis=1), nq - 1)
    live = pos < ends[-1]
    local = jnp.where(live, pos - take(starts, qt), take(cnt, qt) - 1)
    kt = take(lo_t, qt) + local
    first = (live & (local == 0)).astype(jnp.int32)
    last = (live & (local == take(cnt, qt) - 1)).astype(jnp.int32)
    qdoc = take(doc_ids, qblocks)
    kblocks = kt[:, None] * per_k + jnp.arange(per_k, dtype=jnp.int32)[None, :]
    kdoc = take(doc_ids, kblocks)
    qdoc_t = jnp.sum(jnp.where((qt[:, None] == jnp.arange(nq))[:, :, None], qdoc[None], 0), axis=1)
    one_doc = (jnp.min(qdoc_t, axis=1) == jnp.max(qdoc_t, axis=1)) & (
        jnp.min(kdoc, axis=1) == jnp.max(kdoc, axis=1)) & (qdoc_t[:, 0] == kdoc[:, 0])
    below = (kt + 1) * TK - 1 <= take(qstart, qt)
    mode = jnp.where(live, jnp.where(one_doc & below, 2, 1), 0).astype(jnp.int32)
    return (qt.astype(jnp.int32), kt.astype(jnp.int32), first, last, mode, qstart.astype(jnp.int32))


def per_device(queries, keys, values, doc_ids, span_start, span_end, out_weight):
    rows, local_width = queries.shape
    group = lax.axis_size("cl")
    n_cg = lax.axis_size("cg")
    chunk = rows * group
    piece = chunk // n_cg
    j = lax.axis_index("cg")

    stacked = lax.all_to_all(jnp.stack([keys, values]), "cl", 2, 1, tiled=True)
    kv1 = jnp.concatenate([stacked[0], stacked[1]], axis=1)
    kv_all = lax.all_gather(kv1, "cg", axis=0, tiled=True)
    q1 = lax.all_to_all(lax.all_to_all(queries, "cl", 1, 0, tiled=True), "cg", 0, 0, tiled=True)
    seq = kv_all.shape[0]

    count = doc_ids.shape[0]
    span_blocks = block_spans(span_start, span_end, count)
    doc_tok = jnp.broadcast_to(doc_ids[:, None], (count, BLOCK)).reshape(seq)
    span_tok = jnp.broadcast_to(span_blocks[:, None], (count, BLOCK)).reshape(seq)
    key_span = jnp.where(span_tok >= 0, span_tok, -2)
    query_span = jnp.where(span_tok >= 0, span_tok, -1)

    def mine(x):
        return lax.dynamic_index_in_dim(x.reshape(n_cg, n_cg, piece), j, axis=1, keepdims=False).reshape(
            chunk, 1)

    qd = mine(doc_tok)
    qs = mine(query_span)
    kd = doc_tok.reshape(1, seq)
    ks = key_span.reshape(1, seq)
    qstart = jnp.arange(n_cg, dtype=jnp.int32) * chunk + j * piece

    tables = step_tables(doc_ids, span_blocks, span_end, qstart, piece, seq)
    att1 = attend_head(tables, q1, kv_all, qd, qs, kd, ks, piece)
    att0 = lax.all_to_all(att1, "cg", 0, 0, tiled=True)
    attended = lax.all_to_all(att0, "cl", 0, 1, tiled=True)
    tc = lax.axis_index("tc")
    th = lax.axis_index("th")
    swap = [(0, 1), (1, 0)]
    w_other = lax.ppermute(out_weight, "tc", swap)
    w_pair = jnp.where(tc == 0, jnp.concatenate([out_weight, w_other], axis=0),
                       jnp.concatenate([w_other, out_weight], axis=0))
    quarter = rows // 4
    blocks = attended.reshape(2, 2, quarter, local_width)
    keep = lax.dynamic_index_in_dim(blocks, tc, axis=1, keepdims=False)
    give = lax.dynamic_index_in_dim(blocks, 1 - tc, axis=1, keepdims=False)
    got = lax.ppermute(give, "tc", swap)
    a_pair = jnp.where(tc == 0, jnp.concatenate([keep, got], axis=2), jnp.concatenate([got, keep], axis=2))
    a_other = lax.dynamic_index_in_dim(a_pair, 1 - th, axis=0, keepdims=False)
    a_mine = lax.dynamic_index_in_dim(a_pair, th, axis=0, keepdims=False)
    other_half = jnp.dot(a_other, w_pair, preferred_element_type=jnp.float32).astype(jnp.bfloat16)
    recv = lax.ppermute(other_half, "th", swap)
    mine_half = lax.optimization_barrier(jnp.dot(a_mine, w_pair, preferred_element_type=jnp.float32))
    return (mine_half + recv.astype(jnp.float32)).astype(jnp.bfloat16)


def solution(mesh):
    n_ctx = mesh.shape["ctx"]
    group = 4
    inner = Mesh(np.asarray(mesh.devices).reshape(n_ctx // group, group, 2, 2), ("cg", "cl", "th", "tc"))
    out_sharding = NamedSharding(mesh, P(("ctx", "tp"), None))
    split = P(("cg", "cl"), ("th", "tc"))
    body = jax.shard_map(
        per_device,
        mesh=inner,
        in_specs=(split, split, split, P(), P(), P(), P(("th", "tc"), None)),
        out_specs=P(("cg", "cl", "th", "tc"), None),
        check_vma=False,
    )

    def run(*args):
        return lax.with_sharding_constraint(body(*args), out_sharding)

    return run
```

```python
import math

import jax
import jax.numpy as jnp
import numpy as np
from jax import lax
from jax.experimental import pallas as pl
from jax.experimental.pallas import tpu as pltpu
from jax.sharding import Mesh, NamedSharding, PartitionSpec as P

HEAD_DIM = 128
BLOCK = 128
DOC_MOST = 80
SPAN_MOST = 4
TK = 1024

NEG = -1e30


def block_spans(span_start, span_end, count):
    blocks = jnp.arange(count, dtype=jnp.int32)
    inside = (blocks[:, None] >= span_start[None, :]) & (blocks[:, None] < span_end[None, :])
    labels = jnp.arange(1, span_start.shape[0] + 1, dtype=jnp.int32)
    return jnp.sum(jnp.where(inside, labels[None, :], 0), axis=1) - 1


def make_kernel(tq):
    scale = 1.0 / math.sqrt(HEAD_DIM)

    def kernel(qt_ref, kt_ref, first_ref, last_ref, mode_ref, qstart_ref,
               q_ref, k_ref, v_ref, qd_ref, qs_ref, kd_ref, ks_ref, o_ref, m_sc, l_sc, acc_sc):
        p = pl.program_id(0)
        mode = mode_ref[p]

        @pl.when(first_ref[p] == 1)
        def _():
            m_sc[...] = jnp.full(m_sc.shape, NEG, jnp.float32)
            l_sc[...] = jnp.zeros(l_sc.shape, jnp.float32)
            acc_sc[...] = jnp.zeros(acc_sc.shape, jnp.float32)

        def update(masked):
            scores = lax.dot_general(
                q_ref[...], k_ref[...], (((1,), (1,)), ((), ())), preferred_element_type=jnp.float32
            ) * scale
            m_old = m_sc[...]
            if masked:
                qpos = qstart_ref[qt_ref[p]] + lax.broadcasted_iota(jnp.int32, (tq, TK), 0)
                kpos = kt_ref[p] * TK + lax.broadcasted_iota(jnp.int32, (tq, TK), 1)
                allowed = (qd_ref[...] == kd_ref[...]) & ((kpos <= qpos) | (qs_ref[...] == ks_ref[...]))
                scores = jnp.where(allowed, scores, NEG)
                m_new = jnp.maximum(m_old, jnp.max(scores, axis=1, keepdims=True))
                weights = jnp.where(allowed, jnp.exp(scores - m_new), 0.0)
            else:
                m_new = jnp.maximum(m_old, jnp.max(scores, axis=1, keepdims=True))
                weights = jnp.exp(scores - m_new)
            factor = jnp.exp(m_old - m_new)
            l_sc[...] = l_sc[...] * factor + jnp.sum(weights, axis=1, keepdims=True)
            acc_sc[...] = acc_sc[...] * factor + jnp.dot(
                weights.astype(jnp.bfloat16), v_ref[...], preferred_element_type=jnp.float32
            )
            m_sc[...] = m_new

        @pl.when(mode == 1)
        def _():
            update(True)

        @pl.when(mode == 2)
        def _():
            update(False)

        @pl.when(last_ref[p] == 1)
        def _():
            o_ref[...] = (acc_sc[...] / l_sc[...]).astype(o_ref.dtype)

    return kernel


def attend_head(tables, q, kv, qd, qs, kd, ks, tq):
    total = tables[0].shape[0]

    def qmap(p, qt, kt, *_):
        return (qt[p], 0)

    def kmap(p, qt, kt, *_):
        return (kt[p], 0)

    def vmap(p, qt, kt, *_):
        return (kt[p], 1)

    def klab(p, qt, kt, *_):
        return (0, kt[p])

    grid_spec = pltpu.PrefetchScalarGridSpec(
        num_scalar_prefetch=len(tables),
        grid=(total,),
        in_specs=[
            pl.BlockSpec((tq, HEAD_DIM), qmap),
            pl.BlockSpec((TK, HEAD_DIM), kmap),
            pl.BlockSpec((TK, HEAD_DIM), vmap),
            pl.BlockSpec((tq, 1), qmap),
            pl.BlockSpec((tq, 1), qmap),
            pl.BlockSpec((1, TK), klab),
            pl.BlockSpec((1, TK), klab),
        ],
        out_specs=pl.BlockSpec((tq, HEAD_DIM), qmap),
        scratch_shapes=[
            pltpu.VMEM((tq, 1), jnp.float32),
            pltpu.VMEM((tq, 1), jnp.float32),
            pltpu.VMEM((tq, HEAD_DIM), jnp.float32),
        ],
    )
    return pl.pallas_call(
        make_kernel(tq),
        out_shape=jax.ShapeDtypeStruct(q.shape, jnp.bfloat16),
        grid_spec=grid_spec,
        compiler_params=pltpu.CompilerParams(dimension_semantics=("arbitrary",)),
    )(*tables, q, kv, kv, qd, qs, kd, ks)


def take(table, index):
    slots = jnp.arange(table.shape[0], dtype=jnp.int32)
    return jnp.sum(jnp.where(index[..., None] == slots, table, 0), axis=-1)


def step_tables(doc_ids, span_blocks, span_end, qstart, tq, seq):
    count = doc_ids.shape[0]
    nq = qstart.shape[0]
    per_q = tq // BLOCK
    per_k = TK // BLOCK
    ntk = seq // TK
    blocks = jnp.arange(count, dtype=jnp.int32)
    same = doc_ids[:, None] == doc_ids[None, :]
    doc_lo = jnp.min(jnp.where(same, blocks[None, :], count), axis=1)
    doc_hi = jnp.max(jnp.where(same, blocks[None, :], -1), axis=1)
    span_hi = jnp.where(span_blocks >= 0, take(span_end, span_blocks) - 1, blocks)
    key_hi = jnp.minimum(jnp.maximum(span_hi, blocks), doc_hi)
    qblocks = (qstart // BLOCK)[:, None] + jnp.arange(per_q, dtype=jnp.int32)[None, :]
    lo_t = jnp.min(take(doc_lo, qblocks), axis=1) // per_k
    hi_t = jnp.max(take(key_hi, qblocks), axis=1) // per_k
    window = (DOC_MOST - 1) + per_q + (SPAN_MOST - 1)
    most = min(ntk, (window - 1) // per_k + 2)
    cnt = jnp.clip(hi_t - lo_t + 1, 1, most)
    ends = jnp.cumsum(cnt)
    starts = ends - cnt
    stride = seq // nq // BLOCK
    rest, spread = count, 0
    while rest > 0:
        size = min(DOC_MOST, rest)
        spread += sum(max(0, size - 1 - stride * i) for i in range(size // stride + 1))
        rest -= size
    total = min(nq * most, nq * 3 + spread // per_k + 1)
    pos = jnp.arange(total, dtype=jnp.int32)
    qt = jnp.minimum(jnp.sum((pos[:, None] >= ends[None, :]).astype(jnp.int32), axis=1), nq - 1)
    live = pos < ends[-1]
    local = jnp.where(live, pos - take(starts, qt), take(cnt, qt) - 1)
    kt = take(lo_t, qt) + local
    first = (live & (local == 0)).astype(jnp.int32)
    last = (live & (local == take(cnt, qt) - 1)).astype(jnp.int32)
    qdoc = take(doc_ids, qblocks)
    kblocks = kt[:, None] * per_k + jnp.arange(per_k, dtype=jnp.int32)[None, :]
    kdoc = take(doc_ids, kblocks)
    qdoc_t = jnp.sum(jnp.where((qt[:, None] == jnp.arange(nq))[:, :, None], qdoc[None], 0), axis=1)
    one_doc = (jnp.min(qdoc_t, axis=1) == jnp.max(qdoc_t, axis=1)) & (
        jnp.min(kdoc, axis=1) == jnp.max(kdoc, axis=1)) & (qdoc_t[:, 0] == kdoc[:, 0])
    below = (kt + 1) * TK - 1 <= take(qstart, qt)
    mode = jnp.where(live, jnp.where(one_doc & below, 2, 1), 0).astype(jnp.int32)
    return (qt.astype(jnp.int32), kt.astype(jnp.int32), first, last, mode, qstart.astype(jnp.int32))


def per_device(queries, keys, values, doc_ids, span_start, span_end, out_weight):
    rows, local_width = queries.shape
    group = lax.axis_size("cl")
    n_cg = lax.axis_size("cg")
    chunk = rows * group
    piece = chunk // n_cg
    j = lax.axis_index("cg")

    stacked = lax.all_to_all(jnp.stack([keys, values]), "cl", 2, 1, tiled=True)
    kv1 = jnp.concatenate([stacked[0], stacked[1]], axis=1)
    kv_all = lax.all_gather(kv1, "cg", axis=0, tiled=True)
    q1 = lax.all_to_all(lax.all_to_all(queries, "cl", 1, 0, tiled=True), "cg", 0, 0, tiled=True)
    seq = kv_all.shape[0]

    count = doc_ids.shape[0]
    span_blocks = block_spans(span_start, span_end, count)
    doc_tok = jnp.broadcast_to(doc_ids[:, None], (count, BLOCK)).reshape(seq)
    span_tok = jnp.broadcast_to(span_blocks[:, None], (count, BLOCK)).reshape(seq)
    key_span = jnp.where(span_tok >= 0, span_tok, -2)
    query_span = jnp.where(span_tok >= 0, span_tok, -1)

    def mine(x):
        return lax.dynamic_index_in_dim(x.reshape(n_cg, n_cg, piece), j, axis=1, keepdims=False).reshape(
            chunk, 1)

    qd = mine(doc_tok)
    qs = mine(query_span)
    kd = doc_tok.reshape(1, seq)
    ks = key_span.reshape(1, seq)
    qstart = jnp.arange(n_cg, dtype=jnp.int32) * chunk + j * piece

    tables = step_tables(doc_ids, span_blocks, span_end, qstart, piece, seq)
    att1 = attend_head(tables, q1, kv_all, qd, qs, kd, ks, piece)
    att0 = lax.all_to_all(att1, "cg", 0, 0, tiled=True)
    attended = lax.all_to_all(att0, "cl", 0, 1, tiled=True)
    tc = lax.axis_index("tc")
    th = lax.axis_index("th")
    swap = [(0, 1), (1, 0)]
    w_other = lax.ppermute(out_weight, "tc", swap)
    quarter = rows // 4
    blocks = attended.reshape(2, 2, quarter, local_width)
    keep = lax.dynamic_index_in_dim(blocks, tc, axis=1, keepdims=False)
    give = lax.dynamic_index_in_dim(blocks, 1 - tc, axis=1, keepdims=False)
    got = lax.ppermute(give, "tc", swap)

    def project(half):
        own = lax.dynamic_index_in_dim(keep, half, axis=0, keepdims=False)
        other = lax.dynamic_index_in_dim(got, half, axis=0, keepdims=False)
        return jnp.dot(own, out_weight, preferred_element_type=jnp.float32) + jnp.dot(
            other, w_other, preferred_element_type=jnp.float32)

    other_half = project(1 - th).astype(jnp.bfloat16)
    recv = lax.ppermute(other_half, "th", swap)
    mine_half = lax.optimization_barrier(project(th))
    return (mine_half + recv.astype(jnp.float32)).astype(jnp.bfloat16)


def solution(mesh):
    n_ctx = mesh.shape["ctx"]
    group = 4
    inner = Mesh(np.asarray(mesh.devices).reshape(n_ctx // group, group, 2, 2), ("cg", "cl", "th", "tc"))
    out_sharding = NamedSharding(mesh, P(("ctx", "tp"), None))
    split = P(("cg", "cl"), ("th", "tc"))
    body = jax.shard_map(
        per_device,
        mesh=inner,
        in_specs=(split, split, split, P(), P(), P(), P(("th", "tc"), None)),
        out_specs=P(("cg", "cl", "th", "tc"), None),
        check_vma=False,
    )

    def run(*args):
        return lax.with_sharding_constraint(body(*args), out_sharding)

    return run
```

```python
import math

import jax
import jax.numpy as jnp
import numpy as np
from jax import lax
from jax.experimental import pallas as pl
from jax.experimental.pallas import tpu as pltpu
from jax.sharding import Mesh, NamedSharding, PartitionSpec as P

HEAD_DIM = 128
BLOCK = 128
DOC_MOST = 80
SPAN_MOST = 4
TK = 1024

NEG = -1e30
CG = ("cy", "cz")


def block_spans(span_start, span_end, count):
    blocks = jnp.arange(count, dtype=jnp.int32)
    inside = (blocks[:, None] >= span_start[None, :]) & (blocks[:, None] < span_end[None, :])
    labels = jnp.arange(1, span_start.shape[0] + 1, dtype=jnp.int32)
    return jnp.sum(jnp.where(inside, labels[None, :], 0), axis=1) - 1


def make_kernel(tq):
    scale = 1.0 / math.sqrt(HEAD_DIM)

    def kernel(qt_ref, kt_ref, first_ref, last_ref, mode_ref, qstart_ref,
               q_ref, k_ref, v_ref, qd_ref, qs_ref, kd_ref, ks_ref, o_ref, m_sc, l_sc, acc_sc):
        p = pl.program_id(0)
        mode = mode_ref[p]

        @pl.when(first_ref[p] == 1)
        def _():
            m_sc[...] = jnp.full(m_sc.shape, NEG, jnp.float32)
            l_sc[...] = jnp.zeros(l_sc.shape, jnp.float32)
            acc_sc[...] = jnp.zeros(acc_sc.shape, jnp.float32)

        def update(masked):
            scores = lax.dot_general(
                q_ref[...], k_ref[...], (((1,), (1,)), ((), ())), preferred_element_type=jnp.float32
            ) * scale
            m_old = m_sc[...]
            if masked:
                qpos = qstart_ref[qt_ref[p]] + lax.broadcasted_iota(jnp.int32, (tq, TK), 0)
                kpos = kt_ref[p] * TK + lax.broadcasted_iota(jnp.int32, (tq, TK), 1)
                allowed = (qd_ref[...] == kd_ref[...]) & ((kpos <= qpos) | (qs_ref[...] == ks_ref[...]))
                scores = jnp.where(allowed, scores, NEG)
                m_new = jnp.maximum(m_old, jnp.max(scores, axis=1, keepdims=True))
                weights = jnp.where(allowed, jnp.exp(scores - m_new), 0.0)
            else:
                m_new = jnp.maximum(m_old, jnp.max(scores, axis=1, keepdims=True))
                weights = jnp.exp(scores - m_new)
            factor = jnp.exp(m_old - m_new)
            l_sc[...] = l_sc[...] * factor + jnp.sum(weights, axis=1, keepdims=True)
            acc_sc[...] = acc_sc[...] * factor + jnp.dot(
                weights.astype(jnp.bfloat16), v_ref[...], preferred_element_type=jnp.float32
            )
            m_sc[...] = m_new

        @pl.when(mode == 1)
        def _():
            update(True)

        @pl.when(mode == 2)
        def _():
            update(False)

        @pl.when(last_ref[p] == 1)
        def _():
            o_ref[...] = (acc_sc[...] / l_sc[...]).astype(o_ref.dtype)

    return kernel


def attend_head(tables, q, kv, qd, qs, kd, ks, tq):
    total = tables[0].shape[0]

    def qmap(p, qt, kt, *_):
        return (qt[p], 0)

    def kmap(p, qt, kt, *_):
        return (kt[p], 0)

    def vmap(p, qt, kt, *_):
        return (kt[p], 1)

    def klab(p, qt, kt, *_):
        return (0, kt[p])

    grid_spec = pltpu.PrefetchScalarGridSpec(
        num_scalar_prefetch=len(tables),
        grid=(total,),
        in_specs=[
            pl.BlockSpec((tq, HEAD_DIM), qmap),
            pl.BlockSpec((TK, HEAD_DIM), kmap),
            pl.BlockSpec((TK, HEAD_DIM), vmap),
            pl.BlockSpec((tq, 1), qmap),
            pl.BlockSpec((tq, 1), qmap),
            pl.BlockSpec((1, TK), klab),
            pl.BlockSpec((1, TK), klab),
        ],
        out_specs=pl.BlockSpec((tq, HEAD_DIM), qmap),
        scratch_shapes=[
            pltpu.VMEM((tq, 1), jnp.float32),
            pltpu.VMEM((tq, 1), jnp.float32),
            pltpu.VMEM((tq, HEAD_DIM), jnp.float32),
        ],
    )
    return pl.pallas_call(
        make_kernel(tq),
        out_shape=jax.ShapeDtypeStruct(q.shape, jnp.bfloat16),
        grid_spec=grid_spec,
        compiler_params=pltpu.CompilerParams(dimension_semantics=("arbitrary",)),
    )(*tables, q, kv, kv, qd, qs, kd, ks)


def take(table, index):
    slots = jnp.arange(table.shape[0], dtype=jnp.int32)
    return jnp.sum(jnp.where(index[..., None] == slots, table, 0), axis=-1)


def step_tables(doc_ids, span_blocks, span_end, qstart, tq, seq):
    count = doc_ids.shape[0]
    nq = qstart.shape[0]
    per_q = tq // BLOCK
    per_k = TK // BLOCK
    ntk = seq // TK
    blocks = jnp.arange(count, dtype=jnp.int32)
    same = doc_ids[:, None] == doc_ids[None, :]
    doc_lo = jnp.min(jnp.where(same, blocks[None, :], count), axis=1)
    doc_hi = jnp.max(jnp.where(same, blocks[None, :], -1), axis=1)
    span_hi = jnp.where(span_blocks >= 0, take(span_end, span_blocks) - 1, blocks)
    key_hi = jnp.minimum(jnp.maximum(span_hi, blocks), doc_hi)
    qblocks = (qstart // BLOCK)[:, None] + jnp.arange(per_q, dtype=jnp.int32)[None, :]
    lo_t = jnp.min(take(doc_lo, qblocks), axis=1) // per_k
    hi_t = jnp.max(take(key_hi, qblocks), axis=1) // per_k
    window = (DOC_MOST - 1) + per_q + (SPAN_MOST - 1)
    most = min(ntk, (window - 1) // per_k + 2)
    cnt = jnp.clip(hi_t - lo_t + 1, 1, most)
    ends = jnp.cumsum(cnt)
    starts = ends - cnt
    stride = seq // nq // BLOCK
    rest, spread = count, 0
    while rest > 0:
        size = min(DOC_MOST, rest)
        spread += sum(max(0, size - 1 - stride * i) for i in range(size // stride + 1))
        rest -= size
    total = min(nq * most, nq * 3 + spread // per_k + 1)
    pos = jnp.arange(total, dtype=jnp.int32)
    qt = jnp.minimum(jnp.sum((pos[:, None] >= ends[None, :]).astype(jnp.int32), axis=1), nq - 1)
    live = pos < ends[-1]
    local = jnp.where(live, pos - take(starts, qt), take(cnt, qt) - 1)
    kt = take(lo_t, qt) + local
    first = (live & (local == 0)).astype(jnp.int32)
    last = (live & (local == take(cnt, qt) - 1)).astype(jnp.int32)
    qdoc = take(doc_ids, qblocks)
    kblocks = kt[:, None] * per_k + jnp.arange(per_k, dtype=jnp.int32)[None, :]
    kdoc = take(doc_ids, kblocks)
    qdoc_t = jnp.sum(jnp.where((qt[:, None] == jnp.arange(nq))[:, :, None], qdoc[None], 0), axis=1)
    one_doc = (jnp.min(qdoc_t, axis=1) == jnp.max(qdoc_t, axis=1)) & (
        jnp.min(kdoc, axis=1) == jnp.max(kdoc, axis=1)) & (qdoc_t[:, 0] == kdoc[:, 0])
    below = (kt + 1) * TK - 1 <= take(qstart, qt)
    mode = jnp.where(live, jnp.where(one_doc & below, 2, 1), 0).astype(jnp.int32)
    return (qt.astype(jnp.int32), kt.astype(jnp.int32), first, last, mode, qstart.astype(jnp.int32))


def per_device(queries, keys, values, doc_ids, span_start, span_end, out_weight):
    rows, local_width = queries.shape
    group = lax.axis_size("cl")
    n_cg = lax.axis_size(CG)
    chunk = rows * group
    piece = chunk // n_cg
    j = lax.axis_index(CG)

    stacked = lax.all_to_all(jnp.stack([keys, values]), "cl", 2, 1, tiled=True)
    kv1 = jnp.concatenate([stacked[0], stacked[1]], axis=1)
    kv_all = lax.all_gather(lax.all_gather(kv1, "cz", axis=0, tiled=True), "cy", axis=0, tiled=True)
    q1 = lax.all_to_all(lax.all_to_all(queries, "cl", 1, 0, tiled=True), CG, 0, 0, tiled=True)
    seq = kv_all.shape[0]

    count = doc_ids.shape[0]
    span_blocks = block_spans(span_start, span_end, count)
    doc_tok = jnp.broadcast_to(doc_ids[:, None], (count, BLOCK)).reshape(seq)
    span_tok = jnp.broadcast_to(span_blocks[:, None], (count, BLOCK)).reshape(seq)
    key_span = jnp.where(span_tok >= 0, span_tok, -2)
    query_span = jnp.where(span_tok >= 0, span_tok, -1)

    def mine(x):
        return lax.dynamic_index_in_dim(x.reshape(n_cg, n_cg, piece), j, axis=1, keepdims=False).reshape(
            chunk, 1)

    qd = mine(doc_tok)
    qs = mine(query_span)
    kd = doc_tok.reshape(1, seq)
    ks = key_span.reshape(1, seq)
    qstart = jnp.arange(n_cg, dtype=jnp.int32) * chunk + j * piece

    tables = step_tables(doc_ids, span_blocks, span_end, qstart, piece, seq)
    att1 = attend_head(tables, q1, kv_all, qd, qs, kd, ks, piece)
    att0 = lax.all_to_all(att1, CG, 0, 0, tiled=True)
    attended = lax.all_to_all(att0, "cl", 0, 1, tiled=True)
    tc = lax.axis_index("tc")
    th = lax.axis_index("th")
    swap = [(0, 1), (1, 0)]
    w_other = lax.ppermute(out_weight, "tc", swap)
    quarter = rows // 4
    blocks = attended.reshape(2, 2, quarter, local_width)
    keep = lax.dynamic_index_in_dim(blocks, tc, axis=1, keepdims=False)
    give = lax.dynamic_index_in_dim(blocks, 1 - tc, axis=1, keepdims=False)
    got = lax.ppermute(give, "tc", swap)

    def project(half):
        own = lax.dynamic_index_in_dim(keep, half, axis=0, keepdims=False)
        other = lax.dynamic_index_in_dim(got, half, axis=0, keepdims=False)
        return jnp.dot(own, out_weight, preferred_element_type=jnp.float32) + jnp.dot(
            other, w_other, preferred_element_type=jnp.float32)

    other_half = project(1 - th).astype(jnp.bfloat16)
    recv = lax.ppermute(other_half, "th", swap)
    mine_half = lax.optimization_barrier(project(th))
    return (mine_half + recv.astype(jnp.float32)).astype(jnp.bfloat16)


def solution(mesh):
    n_ctx = mesh.shape["ctx"]
    group = 4
    inner = Mesh(np.asarray(mesh.devices).reshape(n_ctx // group // 2, 2, group, 2, 2), ("cy", "cz", "cl", "th", "tc"))
    out_sharding = NamedSharding(mesh, P(("ctx", "tp"), None))
    split = P(("cy", "cz", "cl"), ("th", "tc"))
    body = jax.shard_map(
        per_device,
        mesh=inner,
        in_specs=(split, split, split, P(), P(), P(), P(("th", "tc"), None)),
        out_specs=P(("cy", "cz", "cl", "th", "tc"), None),
        check_vma=False,
    )

    def run(*args):
        return lax.with_sharding_constraint(body(*args), out_sharding)

    return run
```

```python
import math

import jax
import jax.numpy as jnp
import numpy as np
from jax import lax
from jax.experimental import pallas as pl
from jax.experimental.pallas import tpu as pltpu
from jax.sharding import Mesh, NamedSharding, PartitionSpec as P

HEAD_DIM = 128
BLOCK = 128
DOC_MOST = 80
SPAN_MOST = 4
TK = 1024

NEG = -1e30
CG = ("cy", "cx")


def block_spans(span_start, span_end, count):
    blocks = jnp.arange(count, dtype=jnp.int32)
    inside = (blocks[:, None] >= span_start[None, :]) & (blocks[:, None] < span_end[None, :])
    labels = jnp.arange(1, span_start.shape[0] + 1, dtype=jnp.int32)
    return jnp.sum(jnp.where(inside, labels[None, :], 0), axis=1) - 1


def make_kernel(tq):
    scale = 1.0 / math.sqrt(HEAD_DIM)

    def kernel(qt_ref, kt_ref, first_ref, last_ref, mode_ref, qstart_ref,
               q_ref, k_ref, v_ref, qd_ref, qs_ref, kd_ref, ks_ref, o_ref, m_sc, l_sc, acc_sc):
        p = pl.program_id(0)
        mode = mode_ref[p]

        @pl.when(first_ref[p] == 1)
        def _():
            m_sc[...] = jnp.full(m_sc.shape, NEG, jnp.float32)
            l_sc[...] = jnp.zeros(l_sc.shape, jnp.float32)
            acc_sc[...] = jnp.zeros(acc_sc.shape, jnp.float32)

        def update(masked):
            scores = lax.dot_general(
                q_ref[...], k_ref[...], (((1,), (1,)), ((), ())), preferred_element_type=jnp.float32
            ) * scale
            m_old = m_sc[...]
            if masked:
                qpos = qstart_ref[qt_ref[p]] + lax.broadcasted_iota(jnp.int32, (tq, TK), 0)
                kpos = kt_ref[p] * TK + lax.broadcasted_iota(jnp.int32, (tq, TK), 1)
                allowed = (qd_ref[...] == kd_ref[...]) & ((kpos <= qpos) | (qs_ref[...] == ks_ref[...]))
                scores = jnp.where(allowed, scores, NEG)
                m_new = jnp.maximum(m_old, jnp.max(scores, axis=1, keepdims=True))
                weights = jnp.where(allowed, jnp.exp(scores - m_new), 0.0)
            else:
                m_new = jnp.maximum(m_old, jnp.max(scores, axis=1, keepdims=True))
                weights = jnp.exp(scores - m_new)
            factor = jnp.exp(m_old - m_new)
            l_sc[...] = l_sc[...] * factor + jnp.sum(weights, axis=1, keepdims=True)
            acc_sc[...] = acc_sc[...] * factor + jnp.dot(
                weights.astype(jnp.bfloat16), v_ref[...], preferred_element_type=jnp.float32
            )
            m_sc[...] = m_new

        @pl.when(mode == 1)
        def _():
            update(True)

        @pl.when(mode == 2)
        def _():
            update(False)

        @pl.when(last_ref[p] == 1)
        def _():
            o_ref[...] = (acc_sc[...] / l_sc[...]).astype(o_ref.dtype)

    return kernel


def attend_head(tables, q, kv, qd, qs, kd, ks, tq):
    total = tables[0].shape[0]

    def qmap(p, qt, kt, *_):
        return (qt[p], 0)

    def kmap(p, qt, kt, *_):
        return (kt[p], 0)

    def vmap(p, qt, kt, *_):
        return (kt[p], 1)

    def klab(p, qt, kt, *_):
        return (0, kt[p])

    grid_spec = pltpu.PrefetchScalarGridSpec(
        num_scalar_prefetch=len(tables),
        grid=(total,),
        in_specs=[
            pl.BlockSpec((tq, HEAD_DIM), qmap),
            pl.BlockSpec((TK, HEAD_DIM), kmap),
            pl.BlockSpec((TK, HEAD_DIM), vmap),
            pl.BlockSpec((tq, 1), qmap),
            pl.BlockSpec((tq, 1), qmap),
            pl.BlockSpec((1, TK), klab),
            pl.BlockSpec((1, TK), klab),
        ],
        out_specs=pl.BlockSpec((tq, HEAD_DIM), qmap),
        scratch_shapes=[
            pltpu.VMEM((tq, 1), jnp.float32),
            pltpu.VMEM((tq, 1), jnp.float32),
            pltpu.VMEM((tq, HEAD_DIM), jnp.float32),
        ],
    )
    return pl.pallas_call(
        make_kernel(tq),
        out_shape=jax.ShapeDtypeStruct(q.shape, jnp.bfloat16),
        grid_spec=grid_spec,
        compiler_params=pltpu.CompilerParams(dimension_semantics=("arbitrary",)),
    )(*tables, q, kv, kv, qd, qs, kd, ks)


def take(table, index):
    slots = jnp.arange(table.shape[0], dtype=jnp.int32)
    return jnp.sum(jnp.where(index[..., None] == slots, table, 0), axis=-1)


def grid_bound(tiles, count, per_q, per_k, most):
    best = [0] + [-1] * count
    for end in range(1, count + 1):
        for start in range(max(0, end - DOC_MOST), end):
            if best[start] < 0:
                continue
            steps = sum(min(most, (b + per_q + SPAN_MOST - 2) // per_k - start // per_k + 1)
                        for b in tiles if start <= b < end)
            best[end] = max(best[end], best[start] + steps)
    return best[count]


def step_tables(doc_ids, span_blocks, span_end, qstart, tq, seq, layouts):
    count = doc_ids.shape[0]
    nq = qstart.shape[0]
    per_q = tq // BLOCK
    per_k = TK // BLOCK
    ntk = seq // TK
    blocks = jnp.arange(count, dtype=jnp.int32)
    same = doc_ids[:, None] == doc_ids[None, :]
    doc_lo = jnp.min(jnp.where(same, blocks[None, :], count), axis=1)
    doc_hi = jnp.max(jnp.where(same, blocks[None, :], -1), axis=1)
    span_hi = jnp.where(span_blocks >= 0, take(span_end, span_blocks) - 1, blocks)
    key_hi = jnp.minimum(jnp.maximum(span_hi, blocks), doc_hi)
    qblocks = (qstart // BLOCK)[:, None] + jnp.arange(per_q, dtype=jnp.int32)[None, :]
    lo_t = jnp.min(take(doc_lo, qblocks), axis=1) // per_k
    hi_t = jnp.max(take(key_hi, qblocks), axis=1) // per_k
    window = (DOC_MOST - 1) + per_q + (SPAN_MOST - 1)
    most = min(ntk, (window - 1) // per_k + 2)
    cnt = jnp.clip(hi_t - lo_t + 1, 1, most)
    total = min(nq * most, max(grid_bound(tiles, count, per_q, per_k, most) for tiles in layouts))
    ends = jnp.cumsum(cnt)
    starts = ends - cnt
    stride = seq // nq // BLOCK
    rest, spread = count, 0
    while rest > 0:
        size = min(DOC_MOST, rest)
        spread += sum(max(0, size - 1 - stride * i) for i in range(size // stride + 1))
        rest -= size
    total = min(nq * most, nq * 3 + spread // per_k + 1)
    pos = jnp.arange(total, dtype=jnp.int32)
    qt = jnp.minimum(jnp.sum((pos[:, None] >= ends[None, :]).astype(jnp.int32), axis=1), nq - 1)
    live = pos < ends[-1]
    local = jnp.where(live, pos - take(starts, qt), take(cnt, qt) - 1)
    kt = take(lo_t, qt) + local
    first = (live & (local == 0)).astype(jnp.int32)
    last = (live & (local == take(cnt, qt) - 1)).astype(jnp.int32)
    qdoc = take(doc_ids, qblocks)
    kblocks = kt[:, None] * per_k + jnp.arange(per_k, dtype=jnp.int32)[None, :]
    kdoc = take(doc_ids, kblocks)
    qdoc_t = jnp.sum(jnp.where((qt[:, None] == jnp.arange(nq))[:, :, None], qdoc[None], 0), axis=1)
    one_doc = (jnp.min(qdoc_t, axis=1) == jnp.max(qdoc_t, axis=1)) & (
        jnp.min(kdoc, axis=1) == jnp.max(kdoc, axis=1)) & (qdoc_t[:, 0] == kdoc[:, 0])
    below = (kt + 1) * TK - 1 <= take(qstart, qt)
    mode = jnp.where(live, jnp.where(one_doc & below, 2, 1), 0).astype(jnp.int32)
    return (qt.astype(jnp.int32), kt.astype(jnp.int32), first, last, mode, qstart.astype(jnp.int32))


def per_device(queries, keys, values, doc_ids, span_start, span_end, out_weight):
    rows, local_width = queries.shape
    group = lax.axis_size("cl")
    n_cy = lax.axis_size("cy")
    n_cx = lax.axis_size("cx")
    n_cg = n_cy * n_cx
    chunk = rows * group
    piece = chunk // n_cg
    j = lax.axis_index(CG)

    stacked = lax.all_to_all(jnp.stack([keys, values]), "cl", 2, 1, tiled=True)
    kv1 = jnp.concatenate([stacked[0], stacked[1]], axis=1)
    kv_g = lax.all_gather(kv1, CG, axis=0, tiled=True)
    kv_all = kv_g.reshape(n_cy, n_cx, group, rows, 2 * HEAD_DIM).transpose(0, 2, 1, 3, 4).reshape(
        -1, 2 * HEAD_DIM)
    q1 = lax.all_to_all(lax.all_to_all(queries, "cl", 1, 0, tiled=True), CG, 0, 0, tiled=True)
    seq = kv_all.shape[0]

    count = doc_ids.shape[0]
    span_blocks = block_spans(span_start, span_end, count)
    doc_tok = jnp.broadcast_to(doc_ids[:, None], (count, BLOCK)).reshape(seq)
    span_tok = jnp.broadcast_to(span_blocks[:, None], (count, BLOCK)).reshape(seq)
    key_span = jnp.where(span_tok >= 0, span_tok, -2)
    query_span = jnp.where(span_tok >= 0, span_tok, -1)
    halves = rows // piece
    zq = j // halves
    hq = j % halves

    def mine(x):
        x = x.reshape(n_cy, group, n_cx, halves, piece)
        x = lax.dynamic_index_in_dim(x, zq, axis=1, keepdims=False)
        x = lax.dynamic_index_in_dim(x, hq, axis=2, keepdims=False)
        return x.reshape(chunk, 1)

    qd = mine(doc_tok)
    qs = mine(query_span)
    kd = doc_tok.reshape(1, seq)
    ks = key_span.reshape(1, seq)
    g = jnp.arange(n_cg, dtype=jnp.int32)
    qstart = (g // n_cx) * (rows * group * n_cx) + zq * (rows * n_cx) + (g % n_cx) * rows + hq * piece
    qstart = qstart.astype(jnp.int32)

    def first_blocks(jj, gg):
        return ((gg // n_cx) * (rows * group * n_cx) + (jj // halves) * (rows * n_cx) + (gg % n_cx) * rows
                + (jj % halves) * piece) // BLOCK

    layouts = [[first_blocks(jj, gg) for gg in range(n_cg)] for jj in range(n_cg)]
    tables = step_tables(doc_ids, span_blocks, span_end, qstart, piece, seq, layouts)
    att1 = attend_head(tables, q1, kv_all, qd, qs, kd, ks, piece)
    att0 = lax.all_to_all(att1, CG, 0, 0, tiled=True)
    attended = lax.all_to_all(att0, "cl", 0, 1, tiled=True)
    tc = lax.axis_index("tc")
    th = lax.axis_index("th")
    swap = [(0, 1), (1, 0)]
    w_other = lax.ppermute(out_weight, "tc", swap)
    quarter = rows // 4
    blocks = attended.reshape(2, 2, quarter, local_width)
    keep = lax.dynamic_index_in_dim(blocks, tc, axis=1, keepdims=False)
    give = lax.dynamic_index_in_dim(blocks, 1 - tc, axis=1, keepdims=False)
    got = lax.ppermute(give, "tc", swap)

    def project(half):
        own = lax.dynamic_index_in_dim(keep, half, axis=0, keepdims=False)
        other = lax.dynamic_index_in_dim(got, half, axis=0, keepdims=False)
        return jnp.dot(own, out_weight, preferred_element_type=jnp.float32) + jnp.dot(
            other, w_other, preferred_element_type=jnp.float32)

    other_half = project(1 - th).astype(jnp.bfloat16)
    recv = lax.ppermute(other_half, "th", swap)
    mine_half = lax.optimization_barrier(project(th))
    return (mine_half + recv.astype(jnp.float32)).astype(jnp.bfloat16)


def solution(mesh):
    n_ctx = mesh.shape["ctx"]
    group = 4
    inner = Mesh(np.asarray(mesh.devices).reshape(n_ctx // group // 2, group, 2, 2, 2),
                 ("cy", "cl", "cx", "th", "tc"))
    out_sharding = NamedSharding(mesh, P(("ctx", "tp"), None))
    split = P(("cy", "cl", "cx"), ("th", "tc"))
    body = jax.shard_map(
        per_device,
        mesh=inner,
        in_specs=(split, split, split, P(), P(), P(), P(("th", "tc"), None)),
        out_specs=P(("cy", "cl", "cx", "th", "tc"), None),
        check_vma=False,
    )

    def run(*args):
        return lax.with_sharding_constraint(body(*args), out_sharding)

    return run
```

```python
import math

import jax
import jax.numpy as jnp
import numpy as np
from jax import lax
from jax.experimental import pallas as pl
from jax.experimental.pallas import tpu as pltpu
from jax.sharding import Mesh, NamedSharding, PartitionSpec as P

HEAD_DIM = 128
BLOCK = 128
DOC_MOST = 80
SPAN_MOST = 4
TK = 1024

NEG = -1e30


def block_spans(span_start, span_end, count):
    blocks = jnp.arange(count, dtype=jnp.int32)
    inside = (blocks[:, None] >= span_start[None, :]) & (blocks[:, None] < span_end[None, :])
    labels = jnp.arange(1, span_start.shape[0] + 1, dtype=jnp.int32)
    return jnp.sum(jnp.where(inside, labels[None, :], 0), axis=1) - 1


def make_kernel(tq):
    scale = 1.0 / math.sqrt(HEAD_DIM)

    def kernel(qt_ref, kt_ref, first_ref, last_ref, mode_ref, qstart_ref,
               q_ref, k_ref, v_ref, qd_ref, qs_ref, kd_ref, ks_ref, o_ref, m_sc, l_sc, acc_sc):
        p = pl.program_id(0)
        mode = mode_ref[p]

        @pl.when(first_ref[p] == 1)
        def _():
            m_sc[...] = jnp.full(m_sc.shape, NEG, jnp.float32)
            l_sc[...] = jnp.zeros(l_sc.shape, jnp.float32)
            acc_sc[...] = jnp.zeros(acc_sc.shape, jnp.float32)

        def update(masked):
            scores = lax.dot_general(
                q_ref[...], k_ref[...], (((1,), (1,)), ((), ())), preferred_element_type=jnp.float32
            ) * scale
            m_old = m_sc[...]
            if masked:
                qpos = qstart_ref[qt_ref[p]] + lax.broadcasted_iota(jnp.int32, (tq, TK), 0)
                kpos = kt_ref[p] * TK + lax.broadcasted_iota(jnp.int32, (tq, TK), 1)
                allowed = (qd_ref[...] == kd_ref[...]) & ((kpos <= qpos) | (qs_ref[...] == ks_ref[...]))
                scores = jnp.where(allowed, scores, NEG)
                m_new = jnp.maximum(m_old, jnp.max(scores, axis=1, keepdims=True))
                weights = jnp.where(allowed, jnp.exp(scores - m_new), 0.0)
            else:
                m_new = jnp.maximum(m_old, jnp.max(scores, axis=1, keepdims=True))
                weights = jnp.exp(scores - m_new)
            factor = jnp.exp(m_old - m_new)
            l_sc[...] = l_sc[...] * factor + jnp.sum(weights, axis=1, keepdims=True)
            acc_sc[...] = acc_sc[...] * factor + jnp.dot(
                weights.astype(jnp.bfloat16), v_ref[...], preferred_element_type=jnp.float32
            )
            m_sc[...] = m_new

        @pl.when(mode == 1)
        def _():
            update(True)

        @pl.when(mode == 2)
        def _():
            update(False)

        @pl.when(last_ref[p] == 1)
        def _():
            o_ref[...] = (acc_sc[...] / l_sc[...]).astype(o_ref.dtype)

    return kernel


def attend_head(tables, q, kv, qd, qs, kd, ks, tq):
    total = tables[0].shape[0]

    def qmap(p, qt, kt, *_):
        return (qt[p], 0)

    def kmap(p, qt, kt, *_):
        return (kt[p], 0)

    def vmap(p, qt, kt, *_):
        return (kt[p], 1)

    def klab(p, qt, kt, *_):
        return (0, kt[p])

    grid_spec = pltpu.PrefetchScalarGridSpec(
        num_scalar_prefetch=len(tables),
        grid=(total,),
        in_specs=[
            pl.BlockSpec((tq, HEAD_DIM), qmap),
            pl.BlockSpec((TK, HEAD_DIM), kmap),
            pl.BlockSpec((TK, HEAD_DIM), vmap),
            pl.BlockSpec((tq, 1), qmap),
            pl.BlockSpec((tq, 1), qmap),
            pl.BlockSpec((1, TK), klab),
            pl.BlockSpec((1, TK), klab),
        ],
        out_specs=pl.BlockSpec((tq, HEAD_DIM), qmap),
        scratch_shapes=[
            pltpu.VMEM((tq, 1), jnp.float32),
            pltpu.VMEM((tq, 1), jnp.float32),
            pltpu.VMEM((tq, HEAD_DIM), jnp.float32),
        ],
    )
    return pl.pallas_call(
        make_kernel(tq),
        out_shape=jax.ShapeDtypeStruct(q.shape, jnp.bfloat16),
        grid_spec=grid_spec,
        compiler_params=pltpu.CompilerParams(dimension_semantics=("arbitrary",)),
    )(*tables, q, kv, kv, qd, qs, kd, ks)


def take(table, index):
    slots = jnp.arange(table.shape[0], dtype=jnp.int32)
    return jnp.sum(jnp.where(index[..., None] == slots, table, 0), axis=-1)


def grid_bound(tiles, count, per_q, per_k, most):
    best = [0] + [-1] * count
    for end in range(1, count + 1):
        for start in range(max(0, end - DOC_MOST), end):
            if best[start] < 0:
                continue
            steps = sum(min(most, (b + per_q + SPAN_MOST - 2) // per_k - start // per_k + 1)
                        for b in tiles if start <= b < end)
            best[end] = max(best[end], best[start] + steps)
    return best[count]


def step_tables(doc_ids, span_blocks, span_end, qstart, tq, seq, layouts):
    count = doc_ids.shape[0]
    nq = qstart.shape[0]
    per_q = tq // BLOCK
    per_k = TK // BLOCK
    ntk = seq // TK
    blocks = jnp.arange(count, dtype=jnp.int32)
    same = doc_ids[:, None] == doc_ids[None, :]
    doc_lo = jnp.min(jnp.where(same, blocks[None, :], count), axis=1)
    doc_hi = jnp.max(jnp.where(same, blocks[None, :], -1), axis=1)
    span_hi = jnp.where(span_blocks >= 0, take(span_end, span_blocks) - 1, blocks)
    key_hi = jnp.minimum(jnp.maximum(span_hi, blocks), doc_hi)
    qblocks = (qstart // BLOCK)[:, None] + jnp.arange(per_q, dtype=jnp.int32)[None, :]
    lo_t = jnp.min(take(doc_lo, qblocks), axis=1) // per_k
    hi_t = jnp.max(take(key_hi, qblocks), axis=1) // per_k
    window = (DOC_MOST - 1) + per_q + (SPAN_MOST - 1)
    most = min(ntk, (window - 1) // per_k + 2)
    cnt = jnp.clip(hi_t - lo_t + 1, 1, most)
    total = min(nq * most, max(grid_bound(tiles, count, per_q, per_k, most) for tiles in layouts))
    ends = jnp.cumsum(cnt)
    starts = ends - cnt
    pos = jnp.arange(total, dtype=jnp.int32)
    qt = jnp.minimum(jnp.sum((pos[:, None] >= ends[None, :]).astype(jnp.int32), axis=1), nq - 1)
    live = pos < ends[-1]
    local = jnp.where(live, pos - take(starts, qt), take(cnt, qt) - 1)
    kt = take(lo_t, qt) + local
    first = (live & (local == 0)).astype(jnp.int32)
    last = (live & (local == take(cnt, qt) - 1)).astype(jnp.int32)
    qdoc = take(doc_ids, qblocks)
    kblocks = kt[:, None] * per_k + jnp.arange(per_k, dtype=jnp.int32)[None, :]
    kdoc = take(doc_ids, kblocks)
    qdoc_t = jnp.sum(jnp.where((qt[:, None] == jnp.arange(nq))[:, :, None], qdoc[None], 0), axis=1)
    one_doc = (jnp.min(qdoc_t, axis=1) == jnp.max(qdoc_t, axis=1)) & (
        jnp.min(kdoc, axis=1) == jnp.max(kdoc, axis=1)) & (qdoc_t[:, 0] == kdoc[:, 0])
    below = (kt + 1) * TK - 1 <= take(qstart, qt)
    mode = jnp.where(live, jnp.where(one_doc & below, 2, 1), 0).astype(jnp.int32)
    return (qt.astype(jnp.int32), kt.astype(jnp.int32), first, last, mode, qstart.astype(jnp.int32))


def per_device(queries, keys, values, doc_ids, span_start, span_end, out_weight):
    rows, local_width = queries.shape
    group = lax.axis_size("cl")
    n_cg = lax.axis_size("cg")
    chunk = rows * group
    piece = chunk // n_cg
    j = lax.axis_index("cg")

    stacked = lax.all_to_all(jnp.stack([keys, values]), "cl", 2, 1, tiled=True)
    kv1 = jnp.concatenate([stacked[0], stacked[1]], axis=1)
    kv_all = lax.all_gather(kv1, "cg", axis=0, tiled=True)
    q1 = lax.all_to_all(lax.all_to_all(queries, "cl", 1, 0, tiled=True), "cg", 0, 0, tiled=True)
    seq = kv_all.shape[0]

    count = doc_ids.shape[0]
    span_blocks = block_spans(span_start, span_end, count)
    doc_tok = jnp.broadcast_to(doc_ids[:, None], (count, BLOCK)).reshape(seq)
    span_tok = jnp.broadcast_to(span_blocks[:, None], (count, BLOCK)).reshape(seq)
    key_span = jnp.where(span_tok >= 0, span_tok, -2)
    query_span = jnp.where(span_tok >= 0, span_tok, -1)

    def mine(x):
        return lax.dynamic_index_in_dim(x.reshape(n_cg, n_cg, piece), j, axis=1, keepdims=False).reshape(
            chunk, 1)

    qd = mine(doc_tok)
    qs = mine(query_span)
    kd = doc_tok.reshape(1, seq)
    ks = key_span.reshape(1, seq)
    qstart = jnp.arange(n_cg, dtype=jnp.int32) * chunk + j * piece

    layouts = [[(gg * chunk + jj * piece) // BLOCK for gg in range(n_cg)] for jj in range(n_cg)]
    tables = step_tables(doc_ids, span_blocks, span_end, qstart, piece, seq, layouts)
    att1 = attend_head(tables, q1, kv_all, qd, qs, kd, ks, piece)
    att0 = lax.all_to_all(att1, "cg", 0, 0, tiled=True)
    attended = lax.all_to_all(att0, "cl", 0, 1, tiled=True)
    tc = lax.axis_index("tc")
    th = lax.axis_index("th")
    swap = [(0, 1), (1, 0)]
    w_other = lax.ppermute(out_weight, "tc", swap)
    quarter = rows // 4
    blocks = attended.reshape(2, 2, quarter, local_width)
    keep = lax.dynamic_index_in_dim(blocks, tc, axis=1, keepdims=False)
    give = lax.dynamic_index_in_dim(blocks, 1 - tc, axis=1, keepdims=False)
    got = lax.ppermute(give, "tc", swap)

    def project(half):
        own = lax.dynamic_index_in_dim(keep, half, axis=0, keepdims=False)
        other = lax.dynamic_index_in_dim(got, half, axis=0, keepdims=False)
        return jnp.dot(own, out_weight, preferred_element_type=jnp.float32) + jnp.dot(
            other, w_other, preferred_element_type=jnp.float32)

    other_half = project(1 - th).astype(jnp.bfloat16)
    recv = lax.ppermute(other_half, "th", swap)
    mine_half = lax.optimization_barrier(project(th))
    return (mine_half + recv.astype(jnp.float32)).astype(jnp.bfloat16)


def solution(mesh):
    n_ctx = mesh.shape["ctx"]
    group = 4
    inner = Mesh(np.asarray(mesh.devices).reshape(n_ctx // group, group, 2, 2), ("cg", "cl", "th", "tc"))
    out_sharding = NamedSharding(mesh, P(("ctx", "tp"), None))
    split = P(("cg", "cl"), ("th", "tc"))
    body = jax.shard_map(
        per_device,
        mesh=inner,
        in_specs=(split, split, split, P(), P(), P(), P(("th", "tc"), None)),
        out_specs=P(("cg", "cl", "th", "tc"), None),
        check_vma=False,
    )

    def run(*args):
        return lax.with_sharding_constraint(body(*args), out_sharding)

    return run
```

```python
import math

import jax
import jax.numpy as jnp
import numpy as np
from jax import lax
from jax.experimental import pallas as pl
from jax.experimental.pallas import tpu as pltpu
from jax.sharding import Mesh, NamedSharding, PartitionSpec as P

HEAD_DIM = 128
BLOCK = 128
DOC_MOST = 80
SPAN_MOST = 4
TK = 1024

NEG = -1e30


def block_spans(span_start, span_end, count):
    blocks = jnp.arange(count, dtype=jnp.int32)
    inside = (blocks[:, None] >= span_start[None, :]) & (blocks[:, None] < span_end[None, :])
    labels = jnp.arange(1, span_start.shape[0] + 1, dtype=jnp.int32)
    return jnp.sum(jnp.where(inside, labels[None, :], 0), axis=1) - 1


def make_kernel(tq):
    scale = 1.0 / math.sqrt(HEAD_DIM)

    def kernel(qt_ref, kt_ref, first_ref, last_ref, mode_ref, qstart_ref, bdoc_ref, qspan_ref, kspan_ref,
               q_ref, k_ref, v_ref, o_ref, m_sc, l_sc, acc_sc):
        p = pl.program_id(0)
        mode = mode_ref[p]

        @pl.when(first_ref[p] == 1)
        def _():
            m_sc[...] = jnp.full(m_sc.shape, NEG, jnp.float32)
            l_sc[...] = jnp.zeros(l_sc.shape, jnp.float32)
            acc_sc[...] = jnp.zeros(acc_sc.shape, jnp.float32)

        def update(masked):
            scores = lax.dot_general(
                q_ref[...], k_ref[...], (((1,), (1,)), ((), ())), preferred_element_type=jnp.float32
            ) * scale
            m_old = m_sc[...]
            if masked:
                qpos = qstart_ref[qt_ref[p]] + lax.broadcasted_iota(jnp.int32, (tq, TK), 0)
                kpos = kt_ref[p] * TK + lax.broadcasted_iota(jnp.int32, (tq, TK), 1)
                qb0 = qstart_ref[qt_ref[p]] // BLOCK
                kb0 = kt_ref[p] * (TK // BLOCK)
                qrow = lax.broadcasted_iota(jnp.int32, (tq, 1), 0) // BLOCK
                kcol = lax.broadcasted_iota(jnp.int32, (1, TK), 1) // BLOCK
                qd = jnp.zeros((tq, 1), jnp.int32)
                qs = jnp.zeros((tq, 1), jnp.int32)
                for b in range(tq // BLOCK):
                    qd = jnp.where(qrow == b, bdoc_ref[qb0 + b], qd)
                    qs = jnp.where(qrow == b, qspan_ref[qb0 + b], qs)
                kd = jnp.zeros((1, TK), jnp.int32)
                ks = jnp.zeros((1, TK), jnp.int32)
                for b in range(TK // BLOCK):
                    kd = jnp.where(kcol == b, bdoc_ref[kb0 + b], kd)
                    ks = jnp.where(kcol == b, kspan_ref[kb0 + b], ks)
                allowed = (qd == kd) & ((kpos <= qpos) | (qs == ks))
                scores = jnp.where(allowed, scores, NEG)
                m_new = jnp.maximum(m_old, jnp.max(scores, axis=1, keepdims=True))
                weights = jnp.where(allowed, jnp.exp(scores - m_new), 0.0)
            else:
                m_new = jnp.maximum(m_old, jnp.max(scores, axis=1, keepdims=True))
                weights = jnp.exp(scores - m_new)
            factor = jnp.exp(m_old - m_new)
            l_sc[...] = l_sc[...] * factor + jnp.sum(weights, axis=1, keepdims=True)
            acc_sc[...] = acc_sc[...] * factor + jnp.dot(
                weights.astype(jnp.bfloat16), v_ref[...], preferred_element_type=jnp.float32
            )
            m_sc[...] = m_new

        @pl.when(mode == 1)
        def _():
            update(True)

        @pl.when(mode == 2)
        def _():
            update(False)

        @pl.when(last_ref[p] == 1)
        def _():
            o_ref[...] = (acc_sc[...] / l_sc[...]).astype(o_ref.dtype)

    return kernel


def attend_head(tables, q, kv, tq):
    total = tables[0].shape[0]

    def qmap(p, qt, kt, *_):
        return (qt[p], 0)

    def kmap(p, qt, kt, *_):
        return (kt[p], 0)

    def vmap(p, qt, kt, *_):
        return (kt[p], 1)

    def klab(p, qt, kt, *_):
        return (0, kt[p])

    grid_spec = pltpu.PrefetchScalarGridSpec(
        num_scalar_prefetch=len(tables),
        grid=(total,),
        in_specs=[
            pl.BlockSpec((tq, HEAD_DIM), qmap),
            pl.BlockSpec((TK, HEAD_DIM), kmap),
            pl.BlockSpec((TK, HEAD_DIM), vmap),
        ],
        out_specs=pl.BlockSpec((tq, HEAD_DIM), qmap),
        scratch_shapes=[
            pltpu.VMEM((tq, 1), jnp.float32),
            pltpu.VMEM((tq, 1), jnp.float32),
            pltpu.VMEM((tq, HEAD_DIM), jnp.float32),
        ],
    )
    return pl.pallas_call(
        make_kernel(tq),
        out_shape=jax.ShapeDtypeStruct(q.shape, jnp.bfloat16),
        grid_spec=grid_spec,
        compiler_params=pltpu.CompilerParams(dimension_semantics=("arbitrary",)),
    )(*tables, q, kv, kv)


def take(table, index):
    slots = jnp.arange(table.shape[0], dtype=jnp.int32)
    return jnp.sum(jnp.where(index[..., None] == slots, table, 0), axis=-1)


def grid_bound(tiles, count, per_q, per_k, most):
    best = [0] + [-1] * count
    for end in range(1, count + 1):
        for start in range(max(0, end - DOC_MOST), end):
            if best[start] < 0:
                continue
            steps = sum(min(most, (b + per_q + SPAN_MOST - 2) // per_k - start // per_k + 1)
                        for b in tiles if start <= b < end)
            best[end] = max(best[end], best[start] + steps)
    return best[count]


def step_tables(doc_ids, span_blocks, span_end, qstart, tq, seq, layouts):
    count = doc_ids.shape[0]
    nq = qstart.shape[0]
    per_q = tq // BLOCK
    per_k = TK // BLOCK
    ntk = seq // TK
    blocks = jnp.arange(count, dtype=jnp.int32)
    same = doc_ids[:, None] == doc_ids[None, :]
    doc_lo = jnp.min(jnp.where(same, blocks[None, :], count), axis=1)
    doc_hi = jnp.max(jnp.where(same, blocks[None, :], -1), axis=1)
    span_hi = jnp.where(span_blocks >= 0, take(span_end, span_blocks) - 1, blocks)
    key_hi = jnp.minimum(jnp.maximum(span_hi, blocks), doc_hi)
    qblocks = (qstart // BLOCK)[:, None] + jnp.arange(per_q, dtype=jnp.int32)[None, :]
    lo_t = jnp.min(take(doc_lo, qblocks), axis=1) // per_k
    hi_t = jnp.max(take(key_hi, qblocks), axis=1) // per_k
    window = (DOC_MOST - 1) + per_q + (SPAN_MOST - 1)
    most = min(ntk, (window - 1) // per_k + 2)
    cnt = jnp.clip(hi_t - lo_t + 1, 1, most)
    total = min(nq * most, max(grid_bound(tiles, count, per_q, per_k, most) for tiles in layouts))
    ends = jnp.cumsum(cnt)
    starts = ends - cnt
    pos = jnp.arange(total, dtype=jnp.int32)
    qt = jnp.minimum(jnp.sum((pos[:, None] >= ends[None, :]).astype(jnp.int32), axis=1), nq - 1)
    live = pos < ends[-1]
    local = jnp.where(live, pos - take(starts, qt), take(cnt, qt) - 1)
    kt = take(lo_t, qt) + local
    first = (live & (local == 0)).astype(jnp.int32)
    last = (live & (local == take(cnt, qt) - 1)).astype(jnp.int32)
    qdoc = take(doc_ids, qblocks)
    kblocks = kt[:, None] * per_k + jnp.arange(per_k, dtype=jnp.int32)[None, :]
    kdoc = take(doc_ids, kblocks)
    qdoc_t = jnp.sum(jnp.where((qt[:, None] == jnp.arange(nq))[:, :, None], qdoc[None], 0), axis=1)
    one_doc = (jnp.min(qdoc_t, axis=1) == jnp.max(qdoc_t, axis=1)) & (
        jnp.min(kdoc, axis=1) == jnp.max(kdoc, axis=1)) & (qdoc_t[:, 0] == kdoc[:, 0])
    below = (kt + 1) * TK - 1 <= take(qstart, qt)
    mode = jnp.where(live, jnp.where(one_doc & below, 2, 1), 0).astype(jnp.int32)
    return (qt.astype(jnp.int32), kt.astype(jnp.int32), first, last, mode, qstart.astype(jnp.int32))


def per_device(queries, keys, values, doc_ids, span_start, span_end, out_weight):
    rows, local_width = queries.shape
    group = lax.axis_size("cl")
    n_cg = lax.axis_size("cg")
    chunk = rows * group
    piece = chunk // n_cg
    j = lax.axis_index("cg")

    stacked = lax.all_to_all(jnp.stack([keys, values]), "cl", 2, 1, tiled=True)
    kv1 = jnp.concatenate([stacked[0], stacked[1]], axis=1)
    kv_all = lax.all_gather(kv1, "cg", axis=0, tiled=True)
    q1 = lax.all_to_all(lax.all_to_all(queries, "cl", 1, 0, tiled=True), "cg", 0, 0, tiled=True)
    seq = kv_all.shape[0]

    count = doc_ids.shape[0]
    span_blocks = block_spans(span_start, span_end, count)
    doc_tok = jnp.broadcast_to(doc_ids[:, None], (count, BLOCK)).reshape(seq)
    span_tok = jnp.broadcast_to(span_blocks[:, None], (count, BLOCK)).reshape(seq)
    key_span = jnp.where(span_tok >= 0, span_tok, -2)
    query_span = jnp.where(span_tok >= 0, span_tok, -1)

    def mine(x):
        return lax.dynamic_index_in_dim(x.reshape(n_cg, n_cg, piece), j, axis=1, keepdims=False).reshape(
            chunk, 1)

    qd = mine(doc_tok)
    qs = mine(query_span)
    kd = doc_tok.reshape(1, seq)
    ks = key_span.reshape(1, seq)
    qstart = jnp.arange(n_cg, dtype=jnp.int32) * chunk + j * piece

    layouts = [[(gg * chunk + jj * piece) // BLOCK for gg in range(n_cg)] for jj in range(n_cg)]
    tables = step_tables(doc_ids, span_blocks, span_end, qstart, piece, seq, layouts)
    tables = tables + (doc_ids.astype(jnp.int32), jnp.where(span_blocks >= 0, span_blocks, -1).astype(jnp.int32),
                       jnp.where(span_blocks >= 0, span_blocks, -2).astype(jnp.int32))
    att1 = attend_head(tables, q1, kv_all, piece)
    att0 = lax.all_to_all(att1, "cg", 0, 0, tiled=True)
    attended = lax.all_to_all(att0, "cl", 0, 1, tiled=True)
    tc = lax.axis_index("tc")
    th = lax.axis_index("th")
    swap = [(0, 1), (1, 0)]
    w_other = lax.ppermute(out_weight, "tc", swap)
    quarter = rows // 4
    blocks = attended.reshape(2, 2, quarter, local_width)
    keep = lax.dynamic_index_in_dim(blocks, tc, axis=1, keepdims=False)
    give = lax.dynamic_index_in_dim(blocks, 1 - tc, axis=1, keepdims=False)
    got = lax.ppermute(give, "tc", swap)

    def project(half):
        own = lax.dynamic_index_in_dim(keep, half, axis=0, keepdims=False)
        other = lax.dynamic_index_in_dim(got, half, axis=0, keepdims=False)
        return jnp.dot(own, out_weight, preferred_element_type=jnp.float32) + jnp.dot(
            other, w_other, preferred_element_type=jnp.float32)

    other_half = project(1 - th).astype(jnp.bfloat16)
    recv = lax.ppermute(other_half, "th", swap)
    mine_half = lax.optimization_barrier(project(th))
    return (mine_half + recv.astype(jnp.float32)).astype(jnp.bfloat16)


def solution(mesh):
    n_ctx = mesh.shape["ctx"]
    group = 4
    inner = Mesh(np.asarray(mesh.devices).reshape(n_ctx // group, group, 2, 2), ("cg", "cl", "th", "tc"))
    out_sharding = NamedSharding(mesh, P(("ctx", "tp"), None))
    split = P(("cg", "cl"), ("th", "tc"))
    body = jax.shard_map(
        per_device,
        mesh=inner,
        in_specs=(split, split, split, P(), P(), P(), P(("th", "tc"), None)),
        out_specs=P(("cg", "cl", "th", "tc"), None),
        check_vma=False,
    )

    def run(*args):
        return lax.with_sharding_constraint(body(*args), out_sharding)

    return run
```

```python
import math

import jax
import jax.numpy as jnp
import numpy as np
from jax import lax
from jax.experimental import pallas as pl
from jax.experimental.pallas import tpu as pltpu
from jax.sharding import Mesh, NamedSharding, PartitionSpec as P

HEAD_DIM = 128
BLOCK = 128
DOC_MOST = 80
SPAN_MOST = 4
TK = 2048

NEG = -1e30


def block_spans(span_start, span_end, count):
    blocks = jnp.arange(count, dtype=jnp.int32)
    inside = (blocks[:, None] >= span_start[None, :]) & (blocks[:, None] < span_end[None, :])
    labels = jnp.arange(1, span_start.shape[0] + 1, dtype=jnp.int32)
    return jnp.sum(jnp.where(inside, labels[None, :], 0), axis=1) - 1


def make_kernel(tq):
    scale = 1.0 / math.sqrt(HEAD_DIM)

    def kernel(qt_ref, kt_ref, first_ref, last_ref, mode_ref, qstart_ref, bdoc_ref, qspan_ref, kspan_ref,
               q_ref, k_ref, v_ref, o_ref, m_sc, l_sc, acc_sc):
        p = pl.program_id(0)
        mode = mode_ref[p]

        @pl.when(first_ref[p] == 1)
        def _():
            m_sc[...] = jnp.full(m_sc.shape, NEG, jnp.float32)
            l_sc[...] = jnp.zeros(l_sc.shape, jnp.float32)
            acc_sc[...] = jnp.zeros(acc_sc.shape, jnp.float32)

        def update(masked):
            scores = lax.dot_general(
                q_ref[...], k_ref[...], (((1,), (1,)), ((), ())), preferred_element_type=jnp.float32
            ) * scale
            m_old = m_sc[...]
            if masked:
                qpos = qstart_ref[qt_ref[p]] + lax.broadcasted_iota(jnp.int32, (tq, TK), 0)
                kpos = kt_ref[p] * TK + lax.broadcasted_iota(jnp.int32, (tq, TK), 1)
                qb0 = qstart_ref[qt_ref[p]] // BLOCK
                kb0 = kt_ref[p] * (TK // BLOCK)
                qrow = lax.broadcasted_iota(jnp.int32, (tq, 1), 0) // BLOCK
                kcol = lax.broadcasted_iota(jnp.int32, (1, TK), 1) // BLOCK
                qd = jnp.zeros((tq, 1), jnp.int32)
                qs = jnp.zeros((tq, 1), jnp.int32)
                for b in range(tq // BLOCK):
                    qd = jnp.where(qrow == b, bdoc_ref[qb0 + b], qd)
                    qs = jnp.where(qrow == b, qspan_ref[qb0 + b], qs)
                kd = jnp.zeros((1, TK), jnp.int32)
                ks = jnp.zeros((1, TK), jnp.int32)
                for b in range(TK // BLOCK):
                    kd = jnp.where(kcol == b, bdoc_ref[kb0 + b], kd)
                    ks = jnp.where(kcol == b, kspan_ref[kb0 + b], ks)
                allowed = (qd == kd) & ((kpos <= qpos) | (qs == ks))
                scores = jnp.where(allowed, scores, NEG)
                m_new = jnp.maximum(m_old, jnp.max(scores, axis=1, keepdims=True))
                weights = jnp.where(allowed, jnp.exp(scores - m_new), 0.0)
            else:
                m_new = jnp.maximum(m_old, jnp.max(scores, axis=1, keepdims=True))
                weights = jnp.exp(scores - m_new)
            factor = jnp.exp(m_old - m_new)
            l_sc[...] = l_sc[...] * factor + jnp.sum(weights, axis=1, keepdims=True)
            acc_sc[...] = acc_sc[...] * factor + jnp.dot(
                weights.astype(jnp.bfloat16), v_ref[...], preferred_element_type=jnp.float32
            )
            m_sc[...] = m_new

        @pl.when(mode == 1)
        def _():
            update(True)

        @pl.when(mode == 2)
        def _():
            update(False)

        @pl.when(last_ref[p] == 1)
        def _():
            o_ref[...] = (acc_sc[...] / l_sc[...]).astype(o_ref.dtype)

    return kernel


def attend_head(tables, q, kv, tq):
    total = tables[0].shape[0]

    def qmap(p, qt, kt, *_):
        return (qt[p], 0)

    def kmap(p, qt, kt, *_):
        return (kt[p], 0)

    def vmap(p, qt, kt, *_):
        return (kt[p], 1)

    def klab(p, qt, kt, *_):
        return (0, kt[p])

    grid_spec = pltpu.PrefetchScalarGridSpec(
        num_scalar_prefetch=len(tables),
        grid=(total,),
        in_specs=[
            pl.BlockSpec((tq, HEAD_DIM), qmap),
            pl.BlockSpec((TK, HEAD_DIM), kmap),
            pl.BlockSpec((TK, HEAD_DIM), vmap),
        ],
        out_specs=pl.BlockSpec((tq, HEAD_DIM), qmap),
        scratch_shapes=[
            pltpu.VMEM((tq, 1), jnp.float32),
            pltpu.VMEM((tq, 1), jnp.float32),
            pltpu.VMEM((tq, HEAD_DIM), jnp.float32),
        ],
    )
    return pl.pallas_call(
        make_kernel(tq),
        out_shape=jax.ShapeDtypeStruct(q.shape, jnp.bfloat16),
        grid_spec=grid_spec,
        compiler_params=pltpu.CompilerParams(dimension_semantics=("arbitrary",)),
    )(*tables, q, kv, kv)


def take(table, index):
    slots = jnp.arange(table.shape[0], dtype=jnp.int32)
    return jnp.sum(jnp.where(index[..., None] == slots, table, 0), axis=-1)


def grid_bound(tiles, count, per_q, per_k, most):
    best = [0] + [-1] * count
    for end in range(1, count + 1):
        for start in range(max(0, end - DOC_MOST), end):
            if best[start] < 0:
                continue
            steps = sum(min(most, (b + per_q + SPAN_MOST - 2) // per_k - start // per_k + 1)
                        for b in tiles if start <= b < end)
            best[end] = max(best[end], best[start] + steps)
    return best[count]


def step_tables(doc_ids, span_blocks, span_end, qstart, tq, seq, layouts):
    count = doc_ids.shape[0]
    nq = qstart.shape[0]
    per_q = tq // BLOCK
    per_k = TK // BLOCK
    ntk = seq // TK
    blocks = jnp.arange(count, dtype=jnp.int32)
    same = doc_ids[:, None] == doc_ids[None, :]
    doc_lo = jnp.min(jnp.where(same, blocks[None, :], count), axis=1)
    doc_hi = jnp.max(jnp.where(same, blocks[None, :], -1), axis=1)
    span_hi = jnp.where(span_blocks >= 0, take(span_end, span_blocks) - 1, blocks)
    key_hi = jnp.minimum(jnp.maximum(span_hi, blocks), doc_hi)
    qblocks = (qstart // BLOCK)[:, None] + jnp.arange(per_q, dtype=jnp.int32)[None, :]
    lo_t = jnp.min(take(doc_lo, qblocks), axis=1) // per_k
    hi_t = jnp.max(take(key_hi, qblocks), axis=1) // per_k
    window = (DOC_MOST - 1) + per_q + (SPAN_MOST - 1)
    most = min(ntk, (window - 1) // per_k + 2)
    cnt = jnp.clip(hi_t - lo_t + 1, 1, most)
    total = min(nq * most, max(grid_bound(tiles, count, per_q, per_k, most) for tiles in layouts))
    ends = jnp.cumsum(cnt)
    starts = ends - cnt
    pos = jnp.arange(total, dtype=jnp.int32)
    qt = jnp.minimum(jnp.sum((pos[:, None] >= ends[None, :]).astype(jnp.int32), axis=1), nq - 1)
    live = pos < ends[-1]
    local = jnp.where(live, pos - take(starts, qt), take(cnt, qt) - 1)
    kt = take(lo_t, qt) + local
    first = (live & (local == 0)).astype(jnp.int32)
    last = (live & (local == take(cnt, qt) - 1)).astype(jnp.int32)
    qdoc = take(doc_ids, qblocks)
    kblocks = kt[:, None] * per_k + jnp.arange(per_k, dtype=jnp.int32)[None, :]
    kdoc = take(doc_ids, kblocks)
    qdoc_t = jnp.sum(jnp.where((qt[:, None] == jnp.arange(nq))[:, :, None], qdoc[None], 0), axis=1)
    one_doc = (jnp.min(qdoc_t, axis=1) == jnp.max(qdoc_t, axis=1)) & (
        jnp.min(kdoc, axis=1) == jnp.max(kdoc, axis=1)) & (qdoc_t[:, 0] == kdoc[:, 0])
    below = (kt + 1) * TK - 1 <= take(qstart, qt)
    mode = jnp.where(live, jnp.where(one_doc & below, 2, 1), 0).astype(jnp.int32)
    return (qt.astype(jnp.int32), kt.astype(jnp.int32), first, last, mode, qstart.astype(jnp.int32))


def per_device(queries, keys, values, doc_ids, span_start, span_end, out_weight):
    rows, local_width = queries.shape
    group = lax.axis_size("cl")
    n_cg = lax.axis_size("cg")
    chunk = rows * group
    piece = chunk // n_cg
    j = lax.axis_index("cg")

    stacked = lax.all_to_all(jnp.stack([keys, values]), "cl", 2, 1, tiled=True)
    kv1 = jnp.concatenate([stacked[0], stacked[1]], axis=1)
    kv_all = lax.all_gather(kv1, "cg", axis=0, tiled=True)
    q1 = lax.all_to_all(lax.all_to_all(queries, "cl", 1, 0, tiled=True), "cg", 0, 0, tiled=True)
    seq = kv_all.shape[0]

    count = doc_ids.shape[0]
    span_blocks = block_spans(span_start, span_end, count)
    doc_tok = jnp.broadcast_to(doc_ids[:, None], (count, BLOCK)).reshape(seq)
    span_tok = jnp.broadcast_to(span_blocks[:, None], (count, BLOCK)).reshape(seq)
    key_span = jnp.where(span_tok >= 0, span_tok, -2)
    query_span = jnp.where(span_tok >= 0, span_tok, -1)

    def mine(x):
        return lax.dynamic_index_in_dim(x.reshape(n_cg, n_cg, piece), j, axis=1, keepdims=False).reshape(
            chunk, 1)

    qd = mine(doc_tok)
    qs = mine(query_span)
    kd = doc_tok.reshape(1, seq)
    ks = key_span.reshape(1, seq)
    qstart = jnp.arange(n_cg, dtype=jnp.int32) * chunk + j * piece

    layouts = [[(gg * chunk + jj * piece) // BLOCK for gg in range(n_cg)] for jj in range(n_cg)]
    tables = step_tables(doc_ids, span_blocks, span_end, qstart, piece, seq, layouts)
    tables = tables + (doc_ids.astype(jnp.int32), jnp.where(span_blocks >= 0, span_blocks, -1).astype(jnp.int32),
                       jnp.where(span_blocks >= 0, span_blocks, -2).astype(jnp.int32))
    att1 = attend_head(tables, q1, kv_all, piece)
    att0 = lax.all_to_all(att1, "cg", 0, 0, tiled=True)
    attended = lax.all_to_all(att0, "cl", 0, 1, tiled=True)
    tc = lax.axis_index("tc")
    th = lax.axis_index("th")
    swap = [(0, 1), (1, 0)]
    w_other = lax.ppermute(out_weight, "tc", swap)
    quarter = rows // 4
    blocks = attended.reshape(2, 2, quarter, local_width)
    keep = lax.dynamic_index_in_dim(blocks, tc, axis=1, keepdims=False)
    give = lax.dynamic_index_in_dim(blocks, 1 - tc, axis=1, keepdims=False)
    got = lax.ppermute(give, "tc", swap)

    def project(half):
        own = lax.dynamic_index_in_dim(keep, half, axis=0, keepdims=False)
        other = lax.dynamic_index_in_dim(got, half, axis=0, keepdims=False)
        return jnp.dot(own, out_weight, preferred_element_type=jnp.float32) + jnp.dot(
            other, w_other, preferred_element_type=jnp.float32)

    other_half = project(1 - th).astype(jnp.bfloat16)
    recv = lax.ppermute(other_half, "th", swap)
    mine_half = lax.optimization_barrier(project(th))
    return (mine_half + recv.astype(jnp.float32)).astype(jnp.bfloat16)


def solution(mesh):
    n_ctx = mesh.shape["ctx"]
    group = 4
    inner = Mesh(np.asarray(mesh.devices).reshape(n_ctx // group, group, 2, 2), ("cg", "cl", "th", "tc"))
    out_sharding = NamedSharding(mesh, P(("ctx", "tp"), None))
    split = P(("cg", "cl"), ("th", "tc"))
    body = jax.shard_map(
        per_device,
        mesh=inner,
        in_specs=(split, split, split, P(), P(), P(), P(("th", "tc"), None)),
        out_specs=P(("cg", "cl", "th", "tc"), None),
        check_vma=False,
    )

    def run(*args):
        return lax.with_sharding_constraint(body(*args), out_sharding)

    return run
```

```python
import math

import jax
import jax.numpy as jnp
import numpy as np
from jax import lax
from jax.experimental import pallas as pl
from jax.experimental.pallas import tpu as pltpu
from jax.sharding import Mesh, NamedSharding, PartitionSpec as P

HEAD_DIM = 128
BLOCK = 128
DOC_MOST = 80
SPAN_MOST = 4
TK = 1024

NEG = -1e30


def block_spans(span_start, span_end, count):
    blocks = jnp.arange(count, dtype=jnp.int32)
    inside = (blocks[:, None] >= span_start[None, :]) & (blocks[:, None] < span_end[None, :])
    labels = jnp.arange(1, span_start.shape[0] + 1, dtype=jnp.int32)
    return jnp.sum(jnp.where(inside, labels[None, :], 0), axis=1) - 1


def make_kernel(tq):
    scale = 1.0 / math.sqrt(HEAD_DIM)

    def kernel(qt_ref, kt_ref, first_ref, last_ref, mode_ref, qstart_ref, bdoc_ref, qspan_ref, kspan_ref,
               q_ref, k_ref, v_ref, o_ref, m_sc, l_sc, acc_sc):
        p = pl.program_id(0)
        mode = mode_ref[p]

        @pl.when(first_ref[p] == 1)
        def _():
            m_sc[...] = jnp.full(m_sc.shape, NEG, jnp.float32)
            l_sc[...] = jnp.zeros(l_sc.shape, jnp.float32)
            acc_sc[...] = jnp.zeros(acc_sc.shape, jnp.float32)

        def update(masked):
            scores = lax.dot_general(
                q_ref[...], k_ref[...], (((1,), (1,)), ((), ())), preferred_element_type=jnp.float32
            ) * scale
            m_old = m_sc[...]
            if masked:
                qpos = qstart_ref[qt_ref[p]] + lax.broadcasted_iota(jnp.int32, (tq, TK), 0)
                kpos = kt_ref[p] * TK + lax.broadcasted_iota(jnp.int32, (tq, TK), 1)
                qb0 = qstart_ref[qt_ref[p]] // BLOCK
                kb0 = kt_ref[p] * (TK // BLOCK)
                qrow = lax.broadcasted_iota(jnp.int32, (tq, 1), 0) // BLOCK
                kcol = lax.broadcasted_iota(jnp.int32, (1, TK), 1) // BLOCK
                qd = jnp.zeros((tq, 1), jnp.int32)
                qs = jnp.zeros((tq, 1), jnp.int32)
                for b in range(tq // BLOCK):
                    qd = jnp.where(qrow == b, bdoc_ref[qb0 + b], qd)
                    qs = jnp.where(qrow == b, qspan_ref[qb0 + b], qs)
                kd = jnp.zeros((1, TK), jnp.int32)
                ks = jnp.zeros((1, TK), jnp.int32)
                for b in range(TK // BLOCK):
                    kd = jnp.where(kcol == b, bdoc_ref[kb0 + b], kd)
                    ks = jnp.where(kcol == b, kspan_ref[kb0 + b], ks)
                allowed = (qd == kd) & ((kpos <= qpos) | (qs == ks))
                scores = jnp.where(allowed, scores, NEG)
                m_new = jnp.maximum(m_old, jnp.max(scores, axis=1, keepdims=True))
                weights = jnp.where(allowed, jnp.exp(scores - m_new), 0.0)
            else:
                m_new = jnp.maximum(m_old, jnp.max(scores, axis=1, keepdims=True))
                weights = jnp.exp(scores - m_new)
            factor = jnp.exp(m_old - m_new)
            l_sc[...] = l_sc[...] * factor + jnp.sum(weights, axis=1, keepdims=True)
            acc_sc[...] = acc_sc[...] * factor + jnp.dot(
                weights.astype(jnp.bfloat16), v_ref[...], preferred_element_type=jnp.float32
            )
            m_sc[...] = m_new

        @pl.when(mode == 1)
        def _():
            update(True)

        @pl.when(mode == 2)
        def _():
            update(False)

        @pl.when(last_ref[p] == 1)
        def _():
            o_ref[...] = (acc_sc[...] / l_sc[...]).astype(o_ref.dtype)

    return kernel


def attend_head(tables, q, kv, tq):
    total = tables[0].shape[0]

    def qmap(p, qt, kt, *_):
        return (qt[p], 0)

    def kmap(p, qt, kt, *_):
        return (kt[p], 0)

    def vmap(p, qt, kt, *_):
        return (kt[p], 1)

    def klab(p, qt, kt, *_):
        return (0, kt[p])

    grid_spec = pltpu.PrefetchScalarGridSpec(
        num_scalar_prefetch=len(tables),
        grid=(total,),
        in_specs=[
            pl.BlockSpec((tq, HEAD_DIM), qmap),
            pl.BlockSpec((TK, HEAD_DIM), kmap),
            pl.BlockSpec((TK, HEAD_DIM), vmap),
        ],
        out_specs=pl.BlockSpec((tq, HEAD_DIM), qmap),
        scratch_shapes=[
            pltpu.VMEM((tq, 1), jnp.float32),
            pltpu.VMEM((tq, 1), jnp.float32),
            pltpu.VMEM((tq, HEAD_DIM), jnp.float32),
        ],
    )
    return pl.pallas_call(
        make_kernel(tq),
        out_shape=jax.ShapeDtypeStruct(q.shape, jnp.bfloat16),
        grid_spec=grid_spec,
        compiler_params=pltpu.CompilerParams(dimension_semantics=("arbitrary",)),
    )(*tables, q, kv, kv)


def take(table, index):
    slots = jnp.arange(table.shape[0], dtype=jnp.int32)
    return jnp.sum(jnp.where(index[..., None] == slots, table, 0), axis=-1)


def grid_bound(tiles, count, per_q, per_k, most):
    best = [0] + [-1] * count
    for end in range(1, count + 1):
        for start in range(max(0, end - DOC_MOST), end):
            if best[start] < 0:
                continue
            steps = sum(min(most, (b + per_q + SPAN_MOST - 2) // per_k - start // per_k + 1)
                        for b in tiles if start <= b < end)
            best[end] = max(best[end], best[start] + steps)
    return best[count]


def step_tables(doc_ids, span_blocks, span_end, qstart, tq, seq, layouts):
    count = doc_ids.shape[0]
    nq = qstart.shape[0]
    per_q = tq // BLOCK
    per_k = TK // BLOCK
    ntk = seq // TK
    blocks = jnp.arange(count, dtype=jnp.int32)
    same = doc_ids[:, None] == doc_ids[None, :]
    doc_lo = jnp.min(jnp.where(same, blocks[None, :], count), axis=1)
    doc_hi = jnp.max(jnp.where(same, blocks[None, :], -1), axis=1)
    span_hi = jnp.where(span_blocks >= 0, take(span_end, span_blocks) - 1, blocks)
    key_hi = jnp.minimum(jnp.maximum(span_hi, blocks), doc_hi)
    qblocks = (qstart // BLOCK)[:, None] + jnp.arange(per_q, dtype=jnp.int32)[None, :]
    lo_t = jnp.min(take(doc_lo, qblocks), axis=1) // per_k
    hi_t = jnp.max(take(key_hi, qblocks), axis=1) // per_k
    window = (DOC_MOST - 1) + per_q + (SPAN_MOST - 1)
    most = min(ntk, (window - 1) // per_k + 2)
    cnt = jnp.clip(hi_t - lo_t + 1, 1, most)
    total = min(nq * most, max(grid_bound(tiles, count, per_q, per_k, most) for tiles in layouts))
    ends = jnp.cumsum(cnt)
    starts = ends - cnt
    pos = jnp.arange(total, dtype=jnp.int32)
    qt = jnp.minimum(jnp.sum((pos[:, None] >= ends[None, :]).astype(jnp.int32), axis=1), nq - 1)
    live = pos < ends[-1]
    local = jnp.where(live, pos - take(starts, qt), take(cnt, qt) - 1)
    kt = take(lo_t, qt) + local
    first = (live & (local == 0)).astype(jnp.int32)
    last = (live & (local == take(cnt, qt) - 1)).astype(jnp.int32)
    qdoc = take(doc_ids, qblocks)
    kblocks = kt[:, None] * per_k + jnp.arange(per_k, dtype=jnp.int32)[None, :]
    kdoc = take(doc_ids, kblocks)
    qdoc_t = jnp.sum(jnp.where((qt[:, None] == jnp.arange(nq))[:, :, None], qdoc[None], 0), axis=1)
    one_doc = (jnp.min(qdoc_t, axis=1) == jnp.max(qdoc_t, axis=1)) & (
        jnp.min(kdoc, axis=1) == jnp.max(kdoc, axis=1)) & (qdoc_t[:, 0] == kdoc[:, 0])
    below = (kt + 1) * TK - 1 <= take(qstart, qt)
    mode = jnp.where(live, jnp.where(one_doc & below, 2, 1), 0).astype(jnp.int32)
    return (qt.astype(jnp.int32), kt.astype(jnp.int32), first, last, mode, qstart.astype(jnp.int32))


def per_device(queries, keys, values, doc_ids, span_start, span_end, out_weight):
    rows, local_width = queries.shape
    group = lax.axis_size("cl")
    n_cg = lax.axis_size("cg")
    chunk = rows * group
    piece = chunk // n_cg
    j = lax.axis_index("cg")

    stacked = lax.all_to_all(jnp.stack([keys, values]), "cl", 2, 1, tiled=True)
    kv1 = jnp.concatenate([stacked[0], stacked[1]], axis=1)
    kv_all = lax.all_gather(kv1, "cg", axis=0, tiled=True)
    q1 = lax.all_to_all(lax.all_to_all(queries, "cl", 1, 0, tiled=True), "cg", 0, 0, tiled=True)
    seq = kv_all.shape[0]

    count = doc_ids.shape[0]
    span_blocks = block_spans(span_start, span_end, count)
    doc_tok = jnp.broadcast_to(doc_ids[:, None], (count, BLOCK)).reshape(seq)
    span_tok = jnp.broadcast_to(span_blocks[:, None], (count, BLOCK)).reshape(seq)
    key_span = jnp.where(span_tok >= 0, span_tok, -2)
    query_span = jnp.where(span_tok >= 0, span_tok, -1)

    def mine(x):
        return lax.dynamic_index_in_dim(x.reshape(n_cg, n_cg, piece), j, axis=1, keepdims=False).reshape(
            chunk, 1)

    qd = mine(doc_tok)
    qs = mine(query_span)
    kd = doc_tok.reshape(1, seq)
    ks = key_span.reshape(1, seq)
    qstart = jnp.arange(n_cg, dtype=jnp.int32) * chunk + j * piece

    layouts = [[(gg * chunk + jj * piece) // BLOCK for gg in range(n_cg)] for jj in range(n_cg)]
    tables = step_tables(doc_ids, span_blocks, span_end, qstart, piece, seq, layouts)
    tables = tables + (doc_ids.astype(jnp.int32), jnp.where(span_blocks >= 0, span_blocks, -1).astype(jnp.int32),
                       jnp.where(span_blocks >= 0, span_blocks, -2).astype(jnp.int32))
    att1 = attend_head(tables, q1, kv_all, piece)
    att0 = lax.all_to_all(att1, "cg", 0, 0, tiled=True)
    attended = lax.all_to_all(att0, "cl", 0, 1, tiled=True)
    tc = lax.axis_index("tc")
    th = lax.axis_index("th")
    swap = [(0, 1), (1, 0)]
    w_other = lax.ppermute(out_weight, "tc", swap)
    quarter = rows // 4
    blocks = attended.reshape(2, 2, quarter, local_width)
    keep = lax.dynamic_index_in_dim(blocks, tc, axis=1, keepdims=False)
    give = lax.dynamic_index_in_dim(blocks, 1 - tc, axis=1, keepdims=False)
    got = lax.ppermute(give, "tc", swap)

    width = out_weight.shape[1] // 2

    def project(half, col):
        own = lax.dynamic_index_in_dim(keep, half, axis=0, keepdims=False)
        other = lax.dynamic_index_in_dim(got, half, axis=0, keepdims=False)
        w_a = out_weight[:, col * width:(col + 1) * width]
        w_b = w_other[:, col * width:(col + 1) * width]
        return jnp.dot(own, w_a, preferred_element_type=jnp.float32) + jnp.dot(
            other, w_b, preferred_element_type=jnp.float32)

    sent = []
    for col in range(2):
        sent.append(lax.ppermute(project(1 - th, col).astype(jnp.bfloat16), "th", swap))
        if col == 0:
            sent[0] = lax.optimization_barrier(sent[0])
    recv = jnp.concatenate(sent, axis=1)
    mine_half = lax.optimization_barrier(jnp.concatenate([project(th, 0), project(th, 1)], axis=1))
    return (mine_half + recv.astype(jnp.float32)).astype(jnp.bfloat16)


def solution(mesh):
    n_ctx = mesh.shape["ctx"]
    group = 4
    inner = Mesh(np.asarray(mesh.devices).reshape(n_ctx // group, group, 2, 2), ("cg", "cl", "th", "tc"))
    out_sharding = NamedSharding(mesh, P(("ctx", "tp"), None))
    split = P(("cg", "cl"), ("th", "tc"))
    body = jax.shard_map(
        per_device,
        mesh=inner,
        in_specs=(split, split, split, P(), P(), P(), P(("th", "tc"), None)),
        out_specs=P(("cg", "cl", "th", "tc"), None),
        check_vma=False,
    )

    def run(*args):
        return lax.with_sharding_constraint(body(*args), out_sharding)

    return run
```
